32 devices in a mesh: dp: 8 (over y, x, core), space: 4 (over z).
Axes of the slice: x: 2, y: 2, z: 4, core: 2. Of those that a mesh axis runs over, the one named last changes fastest.
Arguments:
- volume: bfloat16 [8, 16, 32, 128], P('dp', 'space'), may hold values from -6 to 6
- first_kernel: bfloat16 [3, 3, 3, 4, 64], replicated, may hold values from -0.625 to 0.625
- mid_kernel: bfloat16 [3, 3, 3, 64, 128], replicated, may hold values from -0.15625 to 0.15625
- deep_kernel: bfloat16 [3, 3, 3, 128, 256], replicated, may hold values from -0.109375 to 0.109375
- deep_cotangent: bfloat16 [8, 8, 16, 16, 256], P('dp', 'space'), may hold values from -6 to 6
Outputs:
- deep_output: bfloat16 [8, 8, 16, 16, 256], P('dp', 'space')
- deep_kernel_grad: float32 [3, 3, 3, 128, 256], P(None, None, None, 'space')
- mid_kernel_grad: float32 [3, 3, 3, 64, 128], replicated
The draws below stay inside these ranges and needn't reach their ends.
All inputs are finite; a program needn't handle non-finite values.
Results may differ from the reference program's by a relative error of at most 0.024.
Values may be sent and summed in bfloat16 or wider, within the bound.
No kernel may reach another device: no remote copies, remote signals or barrier semaphores. Data moves between devices by JAX's collectives and lax.ppermute only.
A program may use at most 128 MiB of HBM per device.

```python
import math
import jax
import jax.numpy as jnp
from jax import lax

CIN = 4
C1 = 64
C2 = 128
C3 = 256
HW = 32
BATCH = 8
DEPTH = 16


def levels(key, extent, pieces, low, top_value):
    level = 1.0
    for dim, shards_of in pieces:
        steps = jax.random.uniform(jax.random.fold_in(jax.random.fold_in(key, 6), dim), (shards_of,), jnp.float32, low / len(pieces), top_value / len(pieces))
        level = level * jnp.repeat(jnp.exp(steps), extent[dim] // shards_of).reshape((-1,) + (1,) * (len(extent) - 1 - dim))
    return level


def centred(rng, extent, spread, most, shards=(), dtype=jnp.bfloat16):
    result = jax.random.normal(rng, extent, jnp.float32) * spread
    if len(shards) > 0:
        result = levels(rng, extent, shards, -0.22, 0.18) * result
    return jnp.clip(result, min=-most, max=most).astype(dtype)


def setup_inputs(seed: int = 0) -> dict:
    splits = jax.random.split(jax.random.key(seed), 6)
    return {
        "volume": centred(splits[0], (BATCH, DEPTH, HW, HW * CIN), 1.0, 6.0, ((0, 8), (1, 4))),
        "first_kernel": centred(splits[1], (3, 3, 3, CIN, C1), (27 * CIN) ** -0.5, 0.625),
        "mid_kernel": centred(splits[2], (3, 3, 3, C1, C2), (27 * C1) ** -0.5, 0.15625),
        "deep_kernel": centred(splits[3], (3, 3, 3, C2, C3), (27 * C2) ** -0.5, 0.109375),
        "deep_cotangent": centred(splits[4], (BATCH, DEPTH // 2, HW // 2, HW // 2, C3), 1.0, 6.0, ((0, 8), (1, 4))),
    }


SLOPE = 0.3
HIGH = lax.Precision.HIGHEST

def activate(value):
    return SLOPE * value + (1.0 - SLOPE) * value * jax.nn.sigmoid(value)

def activate_slope(value):
    sig = jax.nn.sigmoid(value)
    return SLOPE + (1.0 - SLOPE) * (sig + value * sig * (1.0 - sig))

def convolve(values, kernel):
    return lax.conv_general_dilated(values[None], kernel, (1, 1, 1), [(1, 1), (1, 1), (1, 1)], dimension_numbers=('NDHWC', 'DHWIO', 'NDHWC'), precision=HIGH)[0]

def pool_cells(values):
    dd, hh, ww, cc = values.shape
    return values.reshape(dd // 2, 2, hh // 2, 2, ww // 2, 2, cc).mean(axis=(1, 3, 5))

def expand(values):
    return jnp.repeat(jnp.repeat(jnp.repeat(values, 2, 0), 2, 1), 2, 2)

def kernel_grad(padded, cotangent):
    dd, hh, ww, _ = cotangent.shape
    tap_list = []
    for depth_off in range(3):
        for row_off in range(3):
            for col_off in range(3):
                window = padded[depth_off:depth_off + dd, row_off:row_off + hh, col_off:col_off + ww]
                tap_list.append(jnp.einsum('dhwi,dhwo->io', window, cotangent, precision=HIGH))
    return jnp.stack(tap_list).reshape(3, 3, 3, padded.shape[-1], cotangent.shape[-1])

def pad_cells(values):
    return jnp.pad(values, ((1, 1), (1, 1), (1, 1), (0, 0)))

def one_sample(sample, cotangent, first_f, mid_f, deep_f):
    field_in = sample.reshape(DEPTH, HW, HW, CIN).astype(jnp.float32)
    hidden = activate(convolve(field_in, first_f)).astype(jnp.bfloat16)
    pre_mid = convolve(hidden.astype(jnp.float32), mid_f)
    pooled = pool_cells(activate(pre_mid)).astype(jnp.bfloat16)
    pre_deep = convolve(pooled.astype(jnp.float32), deep_f)
    output = activate(pre_deep).astype(jnp.bfloat16)
    grad_pre = (cotangent.astype(jnp.float32) * activate_slope(pre_deep)).astype(jnp.bfloat16)
    deep_term = kernel_grad(pad_cells(pooled.astype(jnp.float32)), grad_pre.astype(jnp.float32))
    flipped = jnp.swapaxes(deep_f[::-1, ::-1, ::-1], 3, 4)
    pooled_grad = convolve(grad_pre.astype(jnp.float32), flipped).astype(jnp.bfloat16)
    grad_mid = (expand(pooled_grad.astype(jnp.float32)) * 0.125 * activate_slope(pre_mid)).astype(jnp.bfloat16)
    mid_term = kernel_grad(pad_cells(hidden.astype(jnp.float32)), grad_mid.astype(jnp.float32))
    return (output, deep_term, mid_term)

def reference(volume, first_kernel, mid_kernel, deep_kernel, deep_cotangent):
    first_f = first_kernel.astype(jnp.float32)
    mid_f = mid_kernel.astype(jnp.float32)
    deep_f = deep_kernel.astype(jnp.float32)

    def sample_step(carry, pair):
        output, deep_term, mid_term = one_sample(pair[0], pair[1], first_f, mid_f, deep_f)
        return ((carry[0] + deep_term, carry[1] + mid_term), output)
    start_sums = (jnp.zeros(deep_kernel.shape, jnp.float32), jnp.zeros(mid_kernel.shape, jnp.float32))
    sums, outputs = lax.scan(sample_step, start_sums, (volume, deep_cotangent))
    deep_scale = math.sqrt(BATCH * (DEPTH // 2) * (HW // 2) * (HW // 2))
    mid_scale = math.sqrt(BATCH * DEPTH * HW * HW)
    return (outputs, sums[0] / deep_scale, sums[1] / mid_scale)
```

```python
import math

import jax
import jax.numpy as jnp
from jax import lax
from jax.sharding import PartitionSpec as P

SLOPE = 0.3


def padded_2(block, sides, width):
    for axis, dim in sides:
        count = lax.axis_size(axis)
        forward = [(i, i + 1) for i in range(count - 1)]
        backward = [(target, source) for source, target in forward]
        low = lax.ppermute(
            lax.slice_in_dim(block, block.shape[dim] - width, None, axis=dim), axis, forward
        )
        high = lax.ppermute(lax.slice_in_dim(block, 0, width, axis=dim), axis, backward)
        block = jnp.concatenate([low, block, high], axis=dim)
    return block


def butterfly_steps(axes):
    steps = []
    for axis in axes:
        count = lax.axis_size(axis)
        bit = 1
        while bit < count:
            steps.append((axis, bit))
            bit *= 2
    return steps


def swap_pairs(axis, bit):
    return [(i, i ^ bit) for i in range(lax.axis_size(axis))]


def gather_depth(block, axis):
    me = lax.axis_index(axis)
    for _, bit in butterfly_steps((axis,)):
        got = lax.ppermute(block, axis, swap_pairs(axis, bit))
        upper = (me // bit) % 2
        block = jnp.where(upper == 0, jnp.concatenate([block, got]), jnp.concatenate([got, block]))
    return block


def reduce_all(rows, axes, wire_dtype):
    steps = butterfly_steps(axes)
    count = rows.shape[0]
    parts = 2 ** len(steps)
    held = jnp.pad(rows, ((0, -count % parts), (0, 0)))
    for axis, bit in steps:
        upper = (lax.axis_index(axis) // bit) % 2
        half = held.shape[0] // 2
        keep = lax.dynamic_slice_in_dim(held, upper * half, half, 0)
        send = lax.dynamic_slice_in_dim(held, (1 - upper) * half, half, 0)
        got = lax.ppermute(send.astype(wire_dtype), axis, swap_pairs(axis, bit))
        held = keep + got.astype(held.dtype)
    held = held.astype(wire_dtype)
    for axis, bit in reversed(steps):
        upper = (lax.axis_index(axis) // bit) % 2
        got = lax.ppermute(held, axis, swap_pairs(axis, bit))
        held = jnp.where(upper == 0, jnp.concatenate([held, got]), jnp.concatenate([got, held]))
    return held[:count].astype(rows.dtype)


def activate(value):
    return SLOPE * value + (1.0 - SLOPE) * value * jax.nn.sigmoid(value)


def activate_slope(value):
    sig = jax.nn.sigmoid(value)
    return SLOPE + (1.0 - SLOPE) * (sig + value * sig * (1.0 - sig))


def conv_depth(padded, kernel):
    return lax.conv_general_dilated(
        padded[None],
        kernel,
        (1, 1, 1),
        [(0, 0), (1, 1), (1, 1)],
        dimension_numbers=("NDHWC", "DHWIO", "NDHWC"),
        preferred_element_type=jnp.float32,
    )[0]


def pool_cells(values):
    dd, hh, ww, cc = values.shape
    return values.reshape(dd // 2, 2, hh // 2, 2, ww // 2, 2, cc).mean(axis=(1, 3, 5))


def expand(values):
    return jnp.repeat(jnp.repeat(jnp.repeat(values, 2, 0), 2, 1), 2, 2)


def kernel_grad(padded, cotangent):
    dd, hh, ww, _ = cotangent.shape
    tap_list = []
    for depth_off in range(3):
        for row_off in range(3):
            for col_off in range(3):
                window = padded[
                    depth_off : depth_off + dd, row_off : row_off + hh, col_off : col_off + ww
                ]
                tap_list.append(
                    jnp.einsum(
                        "dhwi,dhwo->io", window, cotangent, preferred_element_type=jnp.float32
                    )
                )
    return jnp.stack(tap_list).reshape(3, 3, 3, padded.shape[-1], cotangent.shape[-1])


def pad_sides(values):
    return jnp.pad(values, ((0, 0), (1, 1), (1, 1), (0, 0)))


def pad_depth(values):
    return jnp.pad(values, ((1, 1), (0, 0), (0, 0), (0, 0)))


def pad_cells(values):
    return jnp.pad(values, ((1, 1), (1, 1), (1, 1), (0, 0)))


def own_slab(full, slab, space_index):
    return lax.dynamic_slice_in_dim(pad_depth(full), space_index * slab, slab + 2, 0)


def on_device(volume, first_kernel, mid_kernel, deep_kernel, deep_cotangent):
    slab_depth = volume.shape[1]
    side_cells = volume.shape[2]
    in_channels = volume.shape[3] // side_cells
    space_count = lax.axis_size("space")
    space_index = lax.axis_index("space")
    input_field = volume[0].reshape(slab_depth, side_cells, side_cells, in_channels)
    padded = padded_2(input_field, (("space", 0),), 1)
    own_hidden = activate(conv_depth(padded, first_kernel)).astype(jnp.bfloat16)
    hidden = padded_2(own_hidden, (("space", 0),), 1)
    pre_mid = conv_depth(hidden, mid_kernel)
    pooled = pool_cells(activate(pre_mid)).astype(jnp.bfloat16)
    pooled_slab = pooled.shape[0]
    all_pooled = gather_depth(pooled, "space")
    pre_deep = conv_depth(own_slab(all_pooled, pooled_slab, space_index), deep_kernel)
    cotangent = deep_cotangent[0].astype(jnp.float32)
    grad_pre = (cotangent * activate_slope(pre_deep)).astype(jnp.bfloat16)
    all_grad_pre = gather_depth(grad_pre, "space")
    flipped = jnp.swapaxes(deep_kernel[::-1, ::-1, ::-1], 3, 4)
    pooled_grad = conv_depth(own_slab(all_grad_pre, pooled_slab, space_index), flipped).astype(
        jnp.bfloat16
    )
    chan_width = pooled.shape[3] // space_count
    columns = lax.dynamic_slice_in_dim(all_pooled, space_index * chan_width, chan_width, 3)
    deep_term = kernel_grad(pad_cells(columns), all_grad_pre)
    deep_shape = deep_term.shape
    deep_grad = reduce_all(
        deep_term.reshape(-1, deep_shape[-1]), ("dp",), jnp.bfloat16
    ).reshape(deep_shape)
    grad_mid = (expand(pooled_grad.astype(jnp.float32)) * 0.125 * activate_slope(pre_mid)).astype(
        jnp.bfloat16
    )
    mid_term = kernel_grad(pad_sides(hidden), grad_mid)
    mid_shape = mid_term.shape
    mid_grad = reduce_all(
        mid_term.reshape(-1, mid_shape[-1]), ("dp", "space"), jnp.float32
    ).reshape(mid_shape)
    device_total = lax.axis_size("dp") * space_count
    cell_count = slab_depth * side_cells * side_cells
    deep_scale = math.sqrt(device_total * cell_count // 8)
    mid_scale = math.sqrt(device_total * cell_count)
    deep_output = activate(pre_deep).astype(jnp.bfloat16)[None]
    return (deep_output, deep_grad / deep_scale, mid_grad / mid_scale)


def solution(mesh):
    in_specs = (P("dp", "space", None, None), P(), P(), P(), P("dp", "space", None, None, None))
    out_specs = (P("dp", "space", None, None, None), P(None, None, None, "space", None), P())
    return jax.shard_map(
        on_device, mesh=mesh, in_specs=in_specs, out_specs=out_specs, check_vma=False
    )
```

```python
import math

import jax
import jax.numpy as jnp
from jax import lax
from jax.sharding import PartitionSpec as P

SLOPE = 0.3


def padded_2(block, sides, width):
    for axis, dim in sides:
        count = lax.axis_size(axis)
        forward = [(i, i + 1) for i in range(count - 1)]
        backward = [(target, source) for source, target in forward]
        low = lax.ppermute(
            lax.slice_in_dim(block, block.shape[dim] - width, None, axis=dim), axis, forward
        )
        high = lax.ppermute(lax.slice_in_dim(block, 0, width, axis=dim), axis, backward)
        block = jnp.concatenate([low, block, high], axis=dim)
    return block


def digit_groups(axes):
    groups = []
    for axis in axes:
        bits = lax.axis_size(axis).bit_length() - 1
        bit = 1
        if bits % 2 == 1:
            groups.append((axis, 1, 2))
            bit = 2
        while bit < lax.axis_size(axis):
            groups.append((axis, bit, 4))
            bit *= 4
    return groups


def xor_pairs(axis, flip):
    return [(i, i ^ flip) for i in range(lax.axis_size(axis))]


def exchange_parts(block, axis, bit, radix):
    digit = (lax.axis_index(axis) // bit) % radix
    size = block.shape[0]
    out = jnp.zeros((radix * size,) + block.shape[1:], block.dtype)
    out = lax.dynamic_update_slice_in_dim(out, block, digit * size, 0)
    for t in range(1, radix):
        got = lax.ppermute(block, axis, xor_pairs(axis, t * bit))
        out = lax.dynamic_update_slice_in_dim(out, got, (digit ^ t) * size, 0)
    return out


def gather_depth(block, axis):
    for _, bit, radix in digit_groups((axis,)):
        block = exchange_parts(block, axis, bit, radix)
    return block


def gather_columns(block, axis):
    count = lax.axis_size(axis)
    me = lax.axis_index(axis)
    width = block.shape[3] // count
    slab = block.shape[0]
    out = jnp.zeros((count * slab,) + block.shape[1:3] + (width,), block.dtype)
    own = lax.dynamic_slice_in_dim(block, me * width, width, 3)
    out = lax.dynamic_update_slice_in_dim(out, own, me * slab, 0)
    for t in range(1, count):
        part = lax.dynamic_slice_in_dim(block, (me ^ t) * width, width, 3)
        got = lax.ppermute(part, axis, xor_pairs(axis, t))
        out = lax.dynamic_update_slice_in_dim(out, got, (me ^ t) * slab, 0)
    return out


def reduce_all(rows, axes, wire_dtype):
    groups = digit_groups(axes)
    count = rows.shape[0]
    parts = 1
    for _, _, radix in groups:
        parts *= radix
    held = jnp.pad(rows, ((0, -count % parts), (0, 0)))
    for axis, bit, radix in groups:
        digit = (lax.axis_index(axis) // bit) % radix
        size = held.shape[0] // radix
        total = lax.dynamic_slice_in_dim(held, digit * size, size, 0)
        for t in range(1, radix):
            send = lax.dynamic_slice_in_dim(held, (digit ^ t) * size, size, 0)
            got = lax.ppermute(send.astype(wire_dtype), axis, xor_pairs(axis, t * bit))
            total = total + got.astype(held.dtype)
        held = total
    held = held.astype(wire_dtype)
    for axis, bit, radix in reversed(groups):
        held = exchange_parts(held, axis, bit, radix)
    return held[:count].astype(rows.dtype)


def activate(value):
    return SLOPE * value + (1.0 - SLOPE) * value * jax.nn.sigmoid(value)


def activate_slope(value):
    sig = jax.nn.sigmoid(value)
    return SLOPE + (1.0 - SLOPE) * (sig + value * sig * (1.0 - sig))


def conv_depth(padded, kernel):
    return lax.conv_general_dilated(
        padded[None],
        kernel,
        (1, 1, 1),
        [(0, 0), (1, 1), (1, 1)],
        dimension_numbers=("NDHWC", "DHWIO", "NDHWC"),
        preferred_element_type=jnp.float32,
    )[0]


def pool_cells(values):
    dd, hh, ww, cc = values.shape
    return values.reshape(dd // 2, 2, hh // 2, 2, ww // 2, 2, cc).mean(axis=(1, 3, 5))


def expand(values):
    return jnp.repeat(jnp.repeat(jnp.repeat(values, 2, 0), 2, 1), 2, 2)


def kernel_grad(padded, cotangent):
    dd, hh, ww, _ = cotangent.shape
    tap_list = []
    for depth_off in range(3):
        for row_off in range(3):
            for col_off in range(3):
                window = padded[
                    depth_off : depth_off + dd, row_off : row_off + hh, col_off : col_off + ww
                ]
                tap_list.append(
                    jnp.einsum(
                        "dhwi,dhwo->io", window, cotangent, preferred_element_type=jnp.float32
                    )
                )
    return jnp.stack(tap_list).reshape(3, 3, 3, padded.shape[-1], cotangent.shape[-1])


def pad_sides(values):
    return jnp.pad(values, ((0, 0), (1, 1), (1, 1), (0, 0)))


def pad_depth(values):
    return jnp.pad(values, ((1, 1), (0, 0), (0, 0), (0, 0)))


def pad_cells(values):
    return jnp.pad(values, ((1, 1), (1, 1), (1, 1), (0, 0)))


def on_device(volume, first_kernel, mid_kernel, deep_kernel, deep_cotangent):
    slab_depth = volume.shape[1]
    side_cells = volume.shape[2]
    in_channels = volume.shape[3] // side_cells
    space_count = lax.axis_size("space")
    space_index = lax.axis_index("space")
    input_field = volume[0].reshape(slab_depth, side_cells, side_cells, in_channels)
    padded = padded_2(input_field, (("space", 0),), 1)
    own_hidden = activate(conv_depth(padded, first_kernel)).astype(jnp.bfloat16)
    hidden = padded_2(own_hidden, (("space", 0),), 1)
    pre_mid = conv_depth(hidden, mid_kernel)
    pooled = pool_cells(activate(pre_mid)).astype(jnp.bfloat16)
    pre_deep = conv_depth(padded_2(pooled, (("space", 0),), 1), deep_kernel)
    cotangent = deep_cotangent[0].astype(jnp.float32)
    grad_pre = (cotangent * activate_slope(pre_deep)).astype(jnp.bfloat16)
    flipped = jnp.swapaxes(deep_kernel[::-1, ::-1, ::-1], 3, 4)
    pooled_grad = conv_depth(padded_2(grad_pre, (("space", 0),), 1), flipped).astype(jnp.bfloat16)
    columns = gather_columns(pooled, "space")
    all_grad_pre = gather_depth(grad_pre, "space")
    deep_term = kernel_grad(pad_cells(columns), all_grad_pre)
    deep_shape = deep_term.shape
    deep_grad = reduce_all(
        deep_term.reshape(-1, deep_shape[-1]), ("dp",), jnp.bfloat16
    ).reshape(deep_shape)
    grad_mid = (expand(pooled_grad.astype(jnp.float32)) * 0.125 * activate_slope(pre_mid)).astype(
        jnp.bfloat16
    )
    mid_term = kernel_grad(pad_sides(hidden), grad_mid)
    mid_shape = mid_term.shape
    mid_grad = reduce_all(
        mid_term.reshape(-1, mid_shape[-1]), ("dp", "space"), jnp.float32
    ).reshape(mid_shape)
    device_total = lax.axis_size("dp") * space_count
    cell_count = slab_depth * side_cells * side_cells
    deep_scale = math.sqrt(device_total * cell_count // 8)
    mid_scale = math.sqrt(device_total * cell_count)
    deep_output = activate(pre_deep).astype(jnp.bfloat16)[None]
    return (deep_output, deep_grad / deep_scale, mid_grad / mid_scale)


def solution(mesh):
    in_specs = (P("dp", "space", None, None), P(), P(), P(), P("dp", "space", None, None, None))
    out_specs = (P("dp", "space", None, None, None), P(None, None, None, "space", None), P())
    return jax.shard_map(
        on_device, mesh=mesh, in_specs=in_specs, out_specs=out_specs, check_vma=False
    )
```

```python
import math

import jax
import jax.numpy as jnp
from jax import lax
from jax.sharding import PartitionSpec as P

SLOPE = 0.3


def padded_2(block, sides, width):
    for axis, dim in sides:
        count = lax.axis_size(axis)
        forward = [(i, i + 1) for i in range(count - 1)]
        backward = [(target, source) for source, target in forward]
        low = lax.ppermute(
            lax.slice_in_dim(block, block.shape[dim] - width, None, axis=dim), axis, forward
        )
        high = lax.ppermute(lax.slice_in_dim(block, 0, width, axis=dim), axis, backward)
        block = jnp.concatenate([low, block, high], axis=dim)
    return block


def digit_groups(axes):
    groups = []
    for axis in axes:
        bits = lax.axis_size(axis).bit_length() - 1
        bit = 1
        if bits % 2 == 1:
            groups.append((axis, 1, 2))
            bit = 2
        while bit < lax.axis_size(axis):
            groups.append((axis, bit, 4))
            bit *= 4
    return groups


def xor_pairs(axis, flip):
    return [(i, i ^ flip) for i in range(lax.axis_size(axis))]


def exchange_parts(block, axis, bit, radix):
    digit = (lax.axis_index(axis) // bit) % radix
    size = block.shape[0]
    out = jnp.zeros((radix * size,) + block.shape[1:], block.dtype)
    out = lax.dynamic_update_slice_in_dim(out, block, digit * size, 0)
    for t in range(1, radix):
        got = lax.ppermute(block, axis, xor_pairs(axis, t * bit))
        out = lax.dynamic_update_slice_in_dim(out, got, (digit ^ t) * size, 0)
    return out


def gather_depth(block, axis):
    for _, bit, radix in digit_groups((axis,)):
        block = exchange_parts(block, axis, bit, radix)
    return block


def gather_columns(block, axis):
    count = lax.axis_size(axis)
    me = lax.axis_index(axis)
    width = block.shape[3] // count
    slab = block.shape[0]
    out = jnp.zeros((count * slab,) + block.shape[1:3] + (width,), block.dtype)
    own = lax.dynamic_slice_in_dim(block, me * width, width, 3)
    out = lax.dynamic_update_slice_in_dim(out, own, me * slab, 0)
    for t in range(1, count):
        part = lax.dynamic_slice_in_dim(block, (me ^ t) * width, width, 3)
        got = lax.ppermute(part, axis, xor_pairs(axis, t))
        out = lax.dynamic_update_slice_in_dim(out, got, (me ^ t) * slab, 0)
    return out


def reduce_all(rows, axes, wire_dtype):
    groups = digit_groups(axes)
    count = rows.shape[0]
    parts = 1
    for _, _, radix in groups:
        parts *= radix
    held = jnp.pad(rows, ((0, -count % parts), (0, 0)))
    for axis, bit, radix in groups:
        digit = (lax.axis_index(axis) // bit) % radix
        size = held.shape[0] // radix
        total = lax.dynamic_slice_in_dim(held, digit * size, size, 0)
        for t in range(1, radix):
            send = lax.dynamic_slice_in_dim(held, (digit ^ t) * size, size, 0)
            got = lax.ppermute(send.astype(wire_dtype), axis, xor_pairs(axis, t * bit))
            total = total + got.astype(held.dtype)
        held = total
    held = held.astype(wire_dtype)
    for axis, bit, radix in reversed(groups):
        held = exchange_parts(held, axis, bit, radix)
    return held[:count].astype(rows.dtype)


def activate(value):
    return SLOPE * value + (1.0 - SLOPE) * value * jax.nn.sigmoid(value)


def activate_slope(value):
    sig = jax.nn.sigmoid(value)
    return SLOPE + (1.0 - SLOPE) * (sig + value * sig * (1.0 - sig))


def conv_depth(padded, kernel):
    return lax.conv_general_dilated(
        padded[None],
        kernel,
        (1, 1, 1),
        [(0, 0), (1, 1), (1, 1)],
        dimension_numbers=("NDHWC", "DHWIO", "NDHWC"),
        preferred_element_type=jnp.float32,
    )[0]


def pool_cells(values):
    dd, hh, ww, cc = values.shape
    return values.reshape(dd // 2, 2, hh // 2, 2, ww // 2, 2, cc).mean(axis=(1, 3, 5))


def expand(values):
    return jnp.repeat(jnp.repeat(jnp.repeat(values, 2, 0), 2, 1), 2, 2)


def kernel_grad(padded, cotangent):
    dd, hh, ww, _ = cotangent.shape
    tap_list = []
    for depth_off in range(3):
        for row_off in range(3):
            for col_off in range(3):
                window = padded[
                    depth_off : depth_off + dd, row_off : row_off + hh, col_off : col_off + ww
                ]
                tap_list.append(
                    jnp.einsum(
                        "dhwi,dhwo->io", window, cotangent, preferred_element_type=jnp.float32
                    )
                )
    return jnp.stack(tap_list).reshape(3, 3, 3, padded.shape[-1], cotangent.shape[-1])


def pad_sides(values):
    return jnp.pad(values, ((0, 0), (1, 1), (1, 1), (0, 0)))


def pad_depth(values):
    return jnp.pad(values, ((1, 1), (0, 0), (0, 0), (0, 0)))


def pad_cells(values):
    return jnp.pad(values, ((1, 1), (1, 1), (1, 1), (0, 0)))


def banded_kernel(kernel, width):
    taps, cin, cout = kernel.shape[2], kernel.shape[3], kernel.shape[4]
    source = lax.broadcasted_iota(jnp.int32, (taps, width, width), 1)
    target = lax.broadcasted_iota(jnp.int32, (taps, width, width), 2)
    tap = lax.broadcasted_iota(jnp.int32, (taps, width, width), 0)
    select = (source == target + tap - 1).astype(kernel.dtype)
    band = jnp.einsum(
        "tpw,abtco->abpcwo", select, kernel, preferred_element_type=jnp.float32
    ).astype(kernel.dtype)
    return band.reshape(kernel.shape[0], kernel.shape[1], width * cin, width * cout)


def on_device(volume, first_kernel, mid_kernel, deep_kernel, deep_cotangent):
    slab_depth = volume.shape[1]
    side_cells = volume.shape[2]
    space_count = lax.axis_size("space")
    space_index = lax.axis_index("space")
    slab_field = volume[0]
    halo_field = padded_2(slab_field, (("space", 0),), 2)
    banded = banded_kernel(first_kernel, side_cells)
    first_pre = lax.conv_general_dilated(
        halo_field[None],
        banded,
        (1, 1),
        [(0, 0), (1, 1)],
        dimension_numbers=("NHWC", "HWIO", "NHWC"),
        preferred_element_type=jnp.float32,
    )[0]
    plane = space_index * slab_depth - 1 + lax.broadcasted_iota(jnp.int32, first_pre.shape, 0)
    inside = (plane >= 0) & (plane < space_count * slab_depth)
    hidden = jnp.where(inside, activate(first_pre), 0.0).astype(jnp.bfloat16)
    hidden = hidden.reshape(slab_depth + 2, side_cells, side_cells, -1)
    pre_mid = conv_depth(hidden, mid_kernel)
    pooled = pool_cells(activate(pre_mid)).astype(jnp.bfloat16)
    pre_deep = conv_depth(padded_2(pooled, (("space", 0),), 1), deep_kernel)
    cotangent = deep_cotangent[0].astype(jnp.float32)
    grad_pre = (cotangent * activate_slope(pre_deep)).astype(jnp.bfloat16)
    flipped = jnp.swapaxes(deep_kernel[::-1, ::-1, ::-1], 3, 4)
    pooled_grad = conv_depth(padded_2(grad_pre, (("space", 0),), 1), flipped).astype(jnp.bfloat16)
    pooled_late, _ = lax.optimization_barrier((pooled, pre_deep))
    grad_pre_late, _ = lax.optimization_barrier((grad_pre, pooled_grad))
    columns = gather_columns(pooled_late, "space")
    all_grad_pre = gather_depth(grad_pre_late, "space")
    deep_term = kernel_grad(pad_cells(columns), all_grad_pre)
    deep_shape = deep_term.shape
    deep_grad = reduce_all(
        deep_term.reshape(-1, deep_shape[-1]), ("dp",), jnp.bfloat16
    ).reshape(deep_shape)
    grad_mid = (expand(pooled_grad.astype(jnp.float32)) * 0.125 * activate_slope(pre_mid)).astype(
        jnp.bfloat16
    )
    mid_term = kernel_grad(pad_sides(hidden), grad_mid)
    mid_shape = mid_term.shape
    mid_grad = reduce_all(
        mid_term.reshape(-1, mid_shape[-1]), ("dp", "space"), jnp.float32
    ).reshape(mid_shape)
    device_total = lax.axis_size("dp") * space_count
    cell_count = slab_depth * side_cells * side_cells
    deep_scale = math.sqrt(device_total * cell_count // 8)
    mid_scale = math.sqrt(device_total * cell_count)
    deep_output = activate(pre_deep).astype(jnp.bfloat16)[None]
    return (deep_output, deep_grad / deep_scale, mid_grad / mid_scale)


def solution(mesh):
    in_specs = (P("dp", "space", None, None), P(), P(), P(), P("dp", "space", None, None, None))
    out_specs = (P("dp", "space", None, None, None), P(None, None, None, "space", None), P())
    return jax.shard_map(
        on_device, mesh=mesh, in_specs=in_specs, out_specs=out_specs, check_vma=False
    )
```

```python
import math

import jax
import jax.numpy as jnp
from jax import lax
from jax.sharding import PartitionSpec as P

SLOPE = 0.3


def padded_2(block, sides, width):
    for axis, dim in sides:
        count = lax.axis_size(axis)
        forward = [(i, i + 1) for i in range(count - 1)]
        backward = [(target, source) for source, target in forward]
        low = lax.ppermute(
            lax.slice_in_dim(block, block.shape[dim] - width, None, axis=dim), axis, forward
        )
        high = lax.ppermute(lax.slice_in_dim(block, 0, width, axis=dim), axis, backward)
        block = jnp.concatenate([low, block, high], axis=dim)
    return block


def digit_groups(axes):
    groups = []
    for axis in axes:
        bits = lax.axis_size(axis).bit_length() - 1
        bit = 1
        if bits % 2 == 1:
            groups.append((axis, 1, 2))
            bit = 2
        while bit < lax.axis_size(axis):
            groups.append((axis, bit, 4))
            bit *= 4
    return groups


def xor_pairs(axis, flip):
    return [(i, i ^ flip) for i in range(lax.axis_size(axis))]


def exchange_parts(block, axis, bit, radix):
    digit = (lax.axis_index(axis) // bit) % radix
    size = block.shape[0]
    out = jnp.zeros((radix * size,) + block.shape[1:], block.dtype)
    out = lax.dynamic_update_slice_in_dim(out, block, digit * size, 0)
    for t in range(1, radix):
        got = lax.ppermute(block, axis, xor_pairs(axis, t * bit))
        out = lax.dynamic_update_slice_in_dim(out, got, (digit ^ t) * size, 0)
    return out


def gather_depth(block, axis):
    for _, bit, radix in digit_groups((axis,)):
        block = exchange_parts(block, axis, bit, radix)
    return block


def gather_columns(block, axis):
    count = lax.axis_size(axis)
    me = lax.axis_index(axis)
    width = block.shape[3] // count
    slab = block.shape[0]
    out = jnp.zeros((count * slab,) + block.shape[1:3] + (width,), block.dtype)
    own = lax.dynamic_slice_in_dim(block, me * width, width, 3)
    out = lax.dynamic_update_slice_in_dim(out, own, me * slab, 0)
    for t in range(1, count):
        part = lax.dynamic_slice_in_dim(block, (me ^ t) * width, width, 3)
        got = lax.ppermute(part, axis, xor_pairs(axis, t))
        out = lax.dynamic_update_slice_in_dim(out, got, (me ^ t) * slab, 0)
    return out


def reduce_all(rows, axes, wire_dtype):
    groups = digit_groups(axes)
    count = rows.shape[0]
    parts = 1
    for _, _, radix in groups:
        parts *= radix
    held = jnp.pad(rows, ((0, -count % parts), (0, 0)))
    for axis, bit, radix in groups:
        digit = (lax.axis_index(axis) // bit) % radix
        size = held.shape[0] // radix
        total = lax.dynamic_slice_in_dim(held, digit * size, size, 0)
        for t in range(1, radix):
            send = lax.dynamic_slice_in_dim(held, (digit ^ t) * size, size, 0)
            got = lax.ppermute(send.astype(wire_dtype), axis, xor_pairs(axis, t * bit))
            total = total + got.astype(held.dtype)
        held = total
    held = held.astype(wire_dtype)
    for axis, bit, radix in reversed(groups):
        held = exchange_parts(held, axis, bit, radix)
    return held[:count].astype(rows.dtype)


def activate(value):
    return SLOPE * value + (1.0 - SLOPE) * value * jax.nn.sigmoid(value)


def activate_slope(value):
    sig = jax.nn.sigmoid(value)
    return SLOPE + (1.0 - SLOPE) * (sig + value * sig * (1.0 - sig))


def conv_depth(padded, kernel):
    return lax.conv_general_dilated(
        padded[None],
        kernel,
        (1, 1, 1),
        [(0, 0), (1, 1), (1, 1)],
        dimension_numbers=("NDHWC", "DHWIO", "NDHWC"),
        preferred_element_type=jnp.float32,
    )[0]


def pool_cells(values):
    dd, hh, ww, cc = values.shape
    return values.reshape(dd // 2, 2, hh // 2, 2, ww // 2, 2, cc).mean(axis=(1, 3, 5))


def expand(values):
    return jnp.repeat(jnp.repeat(jnp.repeat(values, 2, 0), 2, 1), 2, 2)


def kernel_grad(padded, cotangent):
    out = lax.conv_general_dilated(
        padded[None],
        cotangent[None],
        (1, 1, 1),
        "VALID",
        dimension_numbers=("CDHWN", "IDHWO", "NDHWC"),
        preferred_element_type=jnp.float32,
    )
    return jnp.transpose(out, (1, 2, 3, 0, 4))


def pad_sides(values):
    return jnp.pad(values, ((0, 0), (1, 1), (1, 1), (0, 0)))


def pad_depth(values):
    return jnp.pad(values, ((1, 1), (0, 0), (0, 0), (0, 0)))


def pad_cells(values):
    return jnp.pad(values, ((1, 1), (1, 1), (1, 1), (0, 0)))


def on_device(volume, first_kernel, mid_kernel, deep_kernel, deep_cotangent):
    slab_depth = volume.shape[1]
    side_cells = volume.shape[2]
    in_channels = volume.shape[3] // side_cells
    space_count = lax.axis_size("space")
    space_index = lax.axis_index("space")
    input_field = volume[0].reshape(slab_depth, side_cells, side_cells, in_channels)
    padded = padded_2(input_field, (("space", 0),), 1)
    own_hidden = activate(conv_depth(padded, first_kernel)).astype(jnp.bfloat16)
    hidden = padded_2(own_hidden, (("space", 0),), 1)
    pre_mid = conv_depth(hidden, mid_kernel)
    pooled = pool_cells(activate(pre_mid)).astype(jnp.bfloat16)
    pre_deep = conv_depth(padded_2(pooled, (("space", 0),), 1), deep_kernel)
    pooled, pre_deep = lax.optimization_barrier((pooled, pre_deep))
    cotangent = deep_cotangent[0].astype(jnp.float32)
    grad_pre = (cotangent * activate_slope(pre_deep)).astype(jnp.bfloat16)
    flipped = jnp.swapaxes(deep_kernel[::-1, ::-1, ::-1], 3, 4)
    pooled_grad = conv_depth(padded_2(grad_pre, (("space", 0),), 1), flipped).astype(jnp.bfloat16)
    grad_pre, pooled_grad = lax.optimization_barrier((grad_pre, pooled_grad))
    columns = gather_columns(pooled, "space")
    all_grad_pre = gather_depth(grad_pre, "space")
    deep_term = kernel_grad(pad_cells(columns), all_grad_pre)
    deep_shape = deep_term.shape
    deep_grad = reduce_all(
        deep_term.reshape(-1, deep_shape[-1]), ("dp",), jnp.bfloat16
    ).reshape(deep_shape)
    grad_mid = (expand(pooled_grad.astype(jnp.float32)) * 0.125 * activate_slope(pre_mid)).astype(
        jnp.bfloat16
    )
    mid_term = kernel_grad(pad_sides(hidden), grad_mid)
    mid_shape = mid_term.shape
    mid_grad = reduce_all(
        mid_term.reshape(-1, mid_shape[-1]), ("dp", "space"), jnp.float32
    ).reshape(mid_shape)
    device_total = lax.axis_size("dp") * space_count
    cell_count = slab_depth * side_cells * side_cells
    deep_scale = math.sqrt(device_total * cell_count // 8)
    mid_scale = math.sqrt(device_total * cell_count)
    deep_output = activate(pre_deep).astype(jnp.bfloat16)[None]
    return (deep_output, deep_grad / deep_scale, mid_grad / mid_scale)


def solution(mesh):
    in_specs = (P("dp", "space", None, None), P(), P(), P(), P("dp", "space", None, None, None))
    out_specs = (P("dp", "space", None, None, None), P(None, None, None, "space", None), P())
    return jax.shard_map(
        on_device, mesh=mesh, in_specs=in_specs, out_specs=out_specs, check_vma=False
    )
```

```python
import math

import jax
import jax.numpy as jnp
from jax import lax
from jax.sharding import PartitionSpec as P

SLOPE = 0.3


def padded_2(block, sides, width):
    for axis, dim in sides:
        count = lax.axis_size(axis)
        forward = [(i, i + 1) for i in range(count - 1)]
        backward = [(target, source) for source, target in forward]
        low = lax.ppermute(
            lax.slice_in_dim(block, block.shape[dim] - width, None, axis=dim), axis, forward
        )
        high = lax.ppermute(lax.slice_in_dim(block, 0, width, axis=dim), axis, backward)
        block = jnp.concatenate([low, block, high], axis=dim)
    return block


def digit_groups(axes):
    groups = []
    for axis in axes:
        bits = lax.axis_size(axis).bit_length() - 1
        bit = 1
        if bits % 2 == 1:
            groups.append((axis, 1, 2))
            bit = 2
        while bit < lax.axis_size(axis):
            groups.append((axis, bit, 4))
            bit *= 4
    return groups


def xor_pairs(axis, flip):
    return [(i, i ^ flip) for i in range(lax.axis_size(axis))]


def exchange_parts(block, axis, bit, radix):
    digit = (lax.axis_index(axis) // bit) % radix
    size = block.shape[0]
    out = jnp.zeros((radix * size,) + block.shape[1:], block.dtype)
    out = lax.dynamic_update_slice_in_dim(out, block, digit * size, 0)
    for t in range(1, radix):
        got = lax.ppermute(block, axis, xor_pairs(axis, t * bit))
        out = lax.dynamic_update_slice_in_dim(out, got, (digit ^ t) * size, 0)
    return out


def gather_depth(block, axis):
    for _, bit, radix in digit_groups((axis,)):
        block = exchange_parts(block, axis, bit, radix)
    return block


def gather_columns(block, axis):
    count = lax.axis_size(axis)
    me = lax.axis_index(axis)
    width = block.shape[3] // count
    slab = block.shape[0]
    out = jnp.zeros((count * slab,) + block.shape[1:3] + (width,), block.dtype)
    own = lax.dynamic_slice_in_dim(block, me * width, width, 3)
    out = lax.dynamic_update_slice_in_dim(out, own, me * slab, 0)
    for t in range(1, count):
        part = lax.dynamic_slice_in_dim(block, (me ^ t) * width, width, 3)
        got = lax.ppermute(part, axis, xor_pairs(axis, t))
        out = lax.dynamic_update_slice_in_dim(out, got, (me ^ t) * slab, 0)
    return out


def reduce_all(rows, axes, wire_dtype):
    groups = digit_groups(axes)
    count = rows.shape[0]
    parts = 1
    for _, _, radix in groups:
        parts *= radix
    held = jnp.pad(rows, ((0, -count % parts), (0, 0)))
    for axis, bit, radix in groups:
        digit = (lax.axis_index(axis) // bit) % radix
        size = held.shape[0] // radix
        total = lax.dynamic_slice_in_dim(held, digit * size, size, 0)
        for t in range(1, radix):
            send = lax.dynamic_slice_in_dim(held, (digit ^ t) * size, size, 0)
            got = lax.ppermute(send.astype(wire_dtype), axis, xor_pairs(axis, t * bit))
            total = total + got.astype(held.dtype)
        held = total
    held = held.astype(wire_dtype)
    for axis, bit, radix in reversed(groups):
        held = exchange_parts(held, axis, bit, radix)
    return held[:count].astype(rows.dtype)


def activate(value):
    return SLOPE * value + (1.0 - SLOPE) * value * jax.nn.sigmoid(value)


def activate_slope(value):
    sig = jax.nn.sigmoid(value)
    return SLOPE + (1.0 - SLOPE) * (sig + value * sig * (1.0 - sig))


def conv_depth(padded, kernel):
    return lax.conv_general_dilated(
        padded[None],
        kernel,
        (1, 1, 1),
        [(0, 0), (1, 1), (1, 1)],
        dimension_numbers=("NDHWC", "DHWIO", "NDHWC"),
        preferred_element_type=jnp.float32,
    )[0]


def pool_cells(values):
    dd, hh, ww, cc = values.shape
    return values.reshape(dd // 2, 2, hh // 2, 2, ww // 2, 2, cc).mean(axis=(1, 3, 5))


def expand(values):
    return jnp.repeat(jnp.repeat(jnp.repeat(values, 2, 0), 2, 1), 2, 2)


def kernel_grad(padded, cotangent):
    dd, hh, ww, _ = cotangent.shape
    tap_list = []
    for depth_off in range(3):
        for row_off in range(3):
            for col_off in range(3):
                window = padded[
                    depth_off : depth_off + dd, row_off : row_off + hh, col_off : col_off + ww
                ]
                tap_list.append(
                    jnp.einsum(
                        "dhwi,dhwo->io", window, cotangent, preferred_element_type=jnp.float32
                    )
                )
    return jnp.stack(tap_list).reshape(3, 3, 3, padded.shape[-1], cotangent.shape[-1])


def pad_sides(values):
    return jnp.pad(values, ((0, 0), (1, 1), (1, 1), (0, 0)))


def pad_depth(values):
    return jnp.pad(values, ((1, 1), (0, 0), (0, 0), (0, 0)))


def pad_cells(values):
    return jnp.pad(values, ((1, 1), (1, 1), (1, 1), (0, 0)))


def on_device(volume, first_kernel, mid_kernel, deep_kernel, deep_cotangent):
    slab_depth = volume.shape[1]
    side_cells = volume.shape[2]
    in_channels = volume.shape[3] // side_cells
    space_count = lax.axis_size("space")
    space_index = lax.axis_index("space")
    input_field = volume[0].reshape(slab_depth, side_cells, side_cells, in_channels)
    padded = padded_2(input_field, (("space", 0),), 2)
    first_pre = conv_depth(padded, first_kernel)
    plane = space_index * slab_depth - 1 + lax.broadcasted_iota(jnp.int32, first_pre.shape, 0)
    inside = (plane >= 0) & (plane < space_count * slab_depth)
    hidden = jnp.where(inside, activate(first_pre), 0.0).astype(jnp.bfloat16)
    pre_mid = conv_depth(hidden, mid_kernel)
    pooled = pool_cells(activate(pre_mid)).astype(jnp.bfloat16)
    pre_deep = conv_depth(padded_2(pooled, (("space", 0),), 1), deep_kernel)
    pooled, pre_deep = lax.optimization_barrier((pooled, pre_deep))
    cotangent = deep_cotangent[0].astype(jnp.float32)
    grad_pre = (cotangent * activate_slope(pre_deep)).astype(jnp.bfloat16)
    flipped = jnp.swapaxes(deep_kernel[::-1, ::-1, ::-1], 3, 4)
    pooled_grad = conv_depth(padded_2(grad_pre, (("space", 0),), 1), flipped).astype(jnp.bfloat16)
    grad_pre, pooled_grad = lax.optimization_barrier((grad_pre, pooled_grad))
    columns = gather_columns(pooled, "space")
    all_grad_pre = gather_depth(grad_pre, "space")
    grad_mid = (expand(pooled_grad.astype(jnp.float32)) * 0.125 * activate_slope(pre_mid)).astype(
        jnp.bfloat16
    )
    mid_term = kernel_grad(pad_sides(hidden), grad_mid)
    mid_term, columns, all_grad_pre = lax.optimization_barrier((mid_term, columns, all_grad_pre))
    deep_term = kernel_grad(pad_cells(columns), all_grad_pre)
    deep_shape = deep_term.shape
    deep_grad = reduce_all(
        deep_term.reshape(-1, deep_shape[-1]), ("dp",), jnp.bfloat16
    ).reshape(deep_shape)
    mid_shape = mid_term.shape
    mid_grad = reduce_all(
        mid_term.reshape(-1, mid_shape[-1]), ("dp", "space"), jnp.float32
    ).reshape(mid_shape)
    device_total = lax.axis_size("dp") * space_count
    cell_count = slab_depth * side_cells * side_cells
    deep_scale = math.sqrt(device_total * cell_count // 8)
    mid_scale = math.sqrt(device_total * cell_count)
    deep_output = activate(pre_deep).astype(jnp.bfloat16)[None]
    return (deep_output, deep_grad / deep_scale, mid_grad / mid_scale)


def solution(mesh):
    in_specs = (P("dp", "space", None, None), P(), P(), P(), P("dp", "space", None, None, None))
    out_specs = (P("dp", "space", None, None, None), P(None, None, None, "space", None), P())
    return jax.shard_map(
        on_device, mesh=mesh, in_specs=in_specs, out_specs=out_specs, check_vma=False
    )
```

```python
import math

import jax
import jax.numpy as jnp
from jax import lax
from jax.sharding import PartitionSpec as P

SLOPE = 0.3


def padded_2(block, sides, width):
    for axis, dim in sides:
        count = lax.axis_size(axis)
        forward = [(i, i + 1) for i in range(count - 1)]
        backward = [(target, source) for source, target in forward]
        low = lax.ppermute(
            lax.slice_in_dim(block, block.shape[dim] - width, None, axis=dim), axis, forward
        )
        high = lax.ppermute(lax.slice_in_dim(block, 0, width, axis=dim), axis, backward)
        block = jnp.concatenate([low, block, high], axis=dim)
    return block


def digit_groups(axes):
    groups = []
    for axis in axes:
        bits = lax.axis_size(axis).bit_length() - 1
        bit = 1
        if bits % 2 == 1:
            groups.append((axis, 1, 2))
            bit = 2
        while bit < lax.axis_size(axis):
            groups.append((axis, bit, 4))
            bit *= 4
    return groups


def xor_pairs(axis, flip):
    return [(i, i ^ flip) for i in range(lax.axis_size(axis))]


def exchange_parts(block, axis, bit, radix):
    digit = (lax.axis_index(axis) // bit) % radix
    size = block.shape[0]
    out = jnp.zeros((radix * size,) + block.shape[1:], block.dtype)
    out = lax.dynamic_update_slice_in_dim(out, block, digit * size, 0)
    for t in range(1, radix):
        got = lax.ppermute(block, axis, xor_pairs(axis, t * bit))
        out = lax.dynamic_update_slice_in_dim(out, got, (digit ^ t) * size, 0)
    return out


def gather_depth(block, axis):
    for _, bit, radix in digit_groups((axis,)):
        block = exchange_parts(block, axis, bit, radix)
    return block


def gather_columns(block, axis):
    count = lax.axis_size(axis)
    me = lax.axis_index(axis)
    width = block.shape[3] // count
    slab = block.shape[0]
    out = jnp.zeros((count * slab,) + block.shape[1:3] + (width,), block.dtype)
    own = lax.dynamic_slice_in_dim(block, me * width, width, 3)
    out = lax.dynamic_update_slice_in_dim(out, own, me * slab, 0)
    for t in range(1, count):
        part = lax.dynamic_slice_in_dim(block, (me ^ t) * width, width, 3)
        got = lax.ppermute(part, axis, xor_pairs(axis, t))
        out = lax.dynamic_update_slice_in_dim(out, got, (me ^ t) * slab, 0)
    return out


def reduce_all(rows, axes, wire_dtype, tied=()):
    groups = digit_groups(axes)
    count = rows.shape[0]
    parts = 1
    for _, _, radix in groups:
        parts *= radix
    held = jnp.pad(rows, ((0, -count % parts), (0, 0)))
    for step, (axis, bit, radix) in enumerate(groups):
        digit = (lax.axis_index(axis) // bit) % radix
        size = held.shape[0] // radix
        total = lax.dynamic_slice_in_dim(held, digit * size, size, 0)
        for t in range(1, radix):
            send = lax.dynamic_slice_in_dim(held, (digit ^ t) * size, size, 0)
            got = lax.ppermute(send.astype(wire_dtype), axis, xor_pairs(axis, t * bit))
            total = total + got.astype(held.dtype)
        held = total
        if step == 0:
            held, tied = lax.optimization_barrier((held, tied))
    held = held.astype(wire_dtype)
    for axis, bit, radix in reversed(groups):
        held = exchange_parts(held, axis, bit, radix)
    return held[:count].astype(rows.dtype), tied


def activate(value):
    return SLOPE * value + (1.0 - SLOPE) * value * jax.nn.sigmoid(value)


def activate_slope(value):
    sig = jax.nn.sigmoid(value)
    return SLOPE + (1.0 - SLOPE) * (sig + value * sig * (1.0 - sig))


def conv_depth(padded, kernel):
    return lax.conv_general_dilated(
        padded[None],
        kernel,
        (1, 1, 1),
        [(0, 0), (1, 1), (1, 1)],
        dimension_numbers=("NDHWC", "DHWIO", "NDHWC"),
        preferred_element_type=jnp.float32,
    )[0]


def pool_cells(values):
    dd, hh, ww, cc = values.shape
    return values.reshape(dd // 2, 2, hh // 2, 2, ww // 2, 2, cc).mean(axis=(1, 3, 5))


def expand(values):
    return jnp.repeat(jnp.repeat(jnp.repeat(values, 2, 0), 2, 1), 2, 2)


def kernel_grad(padded, cotangent):
    dd, hh, ww, _ = cotangent.shape
    tap_list = []
    for depth_off in range(3):
        for row_off in range(3):
            for col_off in range(3):
                window = padded[
                    depth_off : depth_off + dd, row_off : row_off + hh, col_off : col_off + ww
                ]
                tap_list.append(
                    jnp.einsum(
                        "dhwi,dhwo->io", window, cotangent, preferred_element_type=jnp.float32
                    )
                )
    return jnp.stack(tap_list).reshape(3, 3, 3, padded.shape[-1], cotangent.shape[-1])


def pad_sides(values):
    return jnp.pad(values, ((0, 0), (1, 1), (1, 1), (0, 0)))


def pad_depth(values):
    return jnp.pad(values, ((1, 1), (0, 0), (0, 0), (0, 0)))


def pad_cells(values):
    return jnp.pad(values, ((1, 1), (1, 1), (1, 1), (0, 0)))


def on_device(volume, first_kernel, mid_kernel, deep_kernel, deep_cotangent):
    slab_depth = volume.shape[1]
    side_cells = volume.shape[2]
    in_channels = volume.shape[3] // side_cells
    space_count = lax.axis_size("space")
    space_index = lax.axis_index("space")
    input_field = volume[0].reshape(slab_depth, side_cells, side_cells, in_channels)
    padded = padded_2(input_field, (("space", 0),), 2)
    first_pre = conv_depth(padded, first_kernel)
    plane = space_index * slab_depth - 1 + jnp.arange(first_pre.shape[0])
    inside = ((plane >= 0) & (plane < space_count * slab_depth)).astype(jnp.float32)
    hidden = (activate(first_pre) * inside[:, None, None, None]).astype(jnp.bfloat16)
    pre_mid = conv_depth(hidden, mid_kernel)
    pooled = pool_cells(activate(pre_mid)).astype(jnp.bfloat16)
    pre_deep = conv_depth(padded_2(pooled, (("space", 0),), 1), deep_kernel)
    pooled, pre_deep = lax.optimization_barrier((pooled, pre_deep))
    cotangent = deep_cotangent[0].astype(jnp.float32)
    grad_pre = (cotangent * activate_slope(pre_deep)).astype(jnp.bfloat16)
    flipped = jnp.swapaxes(deep_kernel[::-1, ::-1, ::-1], 3, 4)
    pooled_grad = conv_depth(padded_2(grad_pre, (("space", 0),), 1), flipped).astype(jnp.bfloat16)
    grad_pre, pooled_grad, pooled = lax.optimization_barrier((grad_pre, pooled_grad, pooled))
    columns = gather_columns(pooled, "space")
    all_grad_pre = gather_depth(grad_pre, "space")
    grad_mid = (expand(pooled_grad.astype(jnp.float32)) * 0.125 * activate_slope(pre_mid)).astype(
        jnp.bfloat16
    )
    mid_term = kernel_grad(pad_sides(hidden), grad_mid)
    mid_shape = mid_term.shape
    mid_grad, (columns, all_grad_pre) = reduce_all(
        mid_term.reshape(-1, mid_shape[-1]), ("dp", "space"), jnp.float32, (columns, all_grad_pre)
    )
    mid_grad = mid_grad.reshape(mid_shape)
    deep_term = kernel_grad(pad_cells(columns), all_grad_pre)
    deep_shape = deep_term.shape
    deep_grad, _ = reduce_all(deep_term.reshape(-1, deep_shape[-1]), ("dp",), jnp.bfloat16)
    deep_grad = deep_grad.reshape(deep_shape)
    device_total = lax.axis_size("dp") * space_count
    cell_count = slab_depth * side_cells * side_cells
    deep_scale = math.sqrt(device_total * cell_count // 8)
    mid_scale = math.sqrt(device_total * cell_count)
    deep_output = activate(pre_deep).astype(jnp.bfloat16)[None]
    return (deep_output, deep_grad / deep_scale, mid_grad / mid_scale)


def solution(mesh):
    in_specs = (P("dp", "space", None, None), P(), P(), P(), P("dp", "space", None, None, None))
    out_specs = (P("dp", "space", None, None, None), P(None, None, None, "space", None), P())
    return jax.shard_map(
        on_device, mesh=mesh, in_specs=in_specs, out_specs=out_specs, check_vma=False
    )
```

```python
import math

import jax
import jax.numpy as jnp
from jax import lax
from jax.sharding import PartitionSpec as P

SLOPE = 0.3


def padded_2(block, sides, width):
    for axis, dim in sides:
        count = lax.axis_size(axis)
        forward = [(i, i + 1) for i in range(count - 1)]
        backward = [(target, source) for source, target in forward]
        low = lax.ppermute(
            lax.slice_in_dim(block, block.shape[dim] - width, None, axis=dim), axis, forward
        )
        high = lax.ppermute(lax.slice_in_dim(block, 0, width, axis=dim), axis, backward)
        block = jnp.concatenate([low, block, high], axis=dim)
    return block


def digit_groups(axes):
    groups = []
    for axis in axes:
        bits = lax.axis_size(axis).bit_length() - 1
        bit = 1
        if bits % 2 == 1:
            groups.append((axis, 1, 2))
            bit = 2
        while bit < lax.axis_size(axis):
            groups.append((axis, bit, 4))
            bit *= 4
    return groups


def xor_pairs(axis, flip):
    return [(i, i ^ flip) for i in range(lax.axis_size(axis))]


def exchange_parts(block, axis, bit, radix):
    digit = (lax.axis_index(axis) // bit) % radix
    size = block.shape[0]
    out = jnp.zeros((radix * size,) + block.shape[1:], block.dtype)
    out = lax.dynamic_update_slice_in_dim(out, block, digit * size, 0)
    for t in range(1, radix):
        got = lax.ppermute(block, axis, xor_pairs(axis, t * bit))
        out = lax.dynamic_update_slice_in_dim(out, got, (digit ^ t) * size, 0)
    return out


def gather_depth(block, axis):
    for _, bit, radix in digit_groups((axis,)):
        block = exchange_parts(block, axis, bit, radix)
    return block


def gather_columns(block, axis):
    count = lax.axis_size(axis)
    me = lax.axis_index(axis)
    width = block.shape[3] // count
    slab = block.shape[0]
    out = jnp.zeros((count * slab,) + block.shape[1:3] + (width,), block.dtype)
    own = lax.dynamic_slice_in_dim(block, me * width, width, 3)
    out = lax.dynamic_update_slice_in_dim(out, own, me * slab, 0)
    for t in range(1, count):
        part = lax.dynamic_slice_in_dim(block, (me ^ t) * width, width, 3)
        got = lax.ppermute(part, axis, xor_pairs(axis, t))
        out = lax.dynamic_update_slice_in_dim(out, got, (me ^ t) * slab, 0)
    return out


def reduce_all(rows, axes, wire_dtype, tied=()):
    groups = digit_groups(axes)
    count = rows.shape[0]
    parts = 1
    for _, _, radix in groups:
        parts *= radix
    held = jnp.pad(rows, ((0, -count % parts), (0, 0)))
    for step, (axis, bit, radix) in enumerate(groups):
        digit = (lax.axis_index(axis) // bit) % radix
        size = held.shape[0] // radix
        total = lax.dynamic_slice_in_dim(held, digit * size, size, 0)
        for t in range(1, radix):
            send = lax.dynamic_slice_in_dim(held, (digit ^ t) * size, size, 0)
            got = lax.ppermute(send.astype(wire_dtype), axis, xor_pairs(axis, t * bit))
            total = total + got.astype(held.dtype)
        held = total
        if step == 0:
            held, tied = lax.optimization_barrier((held, tied))
    held = held.astype(wire_dtype)
    for axis, bit, radix in reversed(groups):
        held = exchange_parts(held, axis, bit, radix)
    return held[:count].astype(rows.dtype), tied


def activate(value):
    return SLOPE * value + (1.0 - SLOPE) * value * jax.nn.sigmoid(value)


def activate_slope(value):
    sig = jax.nn.sigmoid(value)
    return SLOPE + (1.0 - SLOPE) * (sig + value * sig * (1.0 - sig))


def conv_depth(padded, kernel):
    return lax.conv_general_dilated(
        padded[None],
        kernel,
        (1, 1, 1),
        [(0, 0), (1, 1), (1, 1)],
        dimension_numbers=("NDHWC", "DHWIO", "NDHWC"),
        preferred_element_type=jnp.float32,
    )[0]


def pool_cells(values):
    dd, hh, ww, cc = values.shape
    return values.reshape(dd // 2, 2, hh // 2, 2, ww // 2, 2, cc).mean(axis=(1, 3, 5))


def expand(values):
    return jnp.repeat(jnp.repeat(jnp.repeat(values, 2, 0), 2, 1), 2, 2)


def kernel_grad(padded, cotangent):
    dd, hh, ww, _ = cotangent.shape
    tap_list = []
    for depth_off in range(3):
        for row_off in range(3):
            for col_off in range(3):
                window = padded[
                    depth_off : depth_off + dd, row_off : row_off + hh, col_off : col_off + ww
                ]
                tap_list.append(
                    jnp.einsum(
                        "dhwi,dhwo->io", window, cotangent, preferred_element_type=jnp.float32
                    )
                )
    return jnp.stack(tap_list).reshape(3, 3, 3, padded.shape[-1], cotangent.shape[-1])


def pad_sides(values):
    return jnp.pad(values, ((0, 0), (1, 1), (1, 1), (0, 0)))


def pad_depth(values):
    return jnp.pad(values, ((1, 1), (0, 0), (0, 0), (0, 0)))


def pad_cells(values):
    return jnp.pad(values, ((1, 1), (1, 1), (1, 1), (0, 0)))


def first_layer(padded, kernel):
    dd, hh, ww, _ = padded.shape
    sides = pad_sides(padded)
    taps = [
        sides[a : a + dd - 2, b : b + hh, c : c + ww]
        for a in range(3)
        for b in range(3)
        for c in range(3)
    ]
    patches = jnp.concatenate(taps, axis=-1)
    flat_kernel = kernel.reshape(-1, kernel.shape[-1])
    return jnp.einsum("dhwk,ko->dhwo", patches, flat_kernel, preferred_element_type=jnp.float32)


def on_device(volume, first_kernel, mid_kernel, deep_kernel, deep_cotangent):
    slab_depth = volume.shape[1]
    side_cells = volume.shape[2]
    in_channels = volume.shape[3] // side_cells
    space_count = lax.axis_size("space")
    space_index = lax.axis_index("space")
    input_field = volume[0].reshape(slab_depth, side_cells, side_cells, in_channels)
    padded = padded_2(input_field, (("space", 0),), 2)
    first_pre = first_layer(padded, first_kernel)
    plane = space_index * slab_depth - 1 + jnp.arange(first_pre.shape[0])
    inside = ((plane >= 0) & (plane < space_count * slab_depth)).astype(jnp.float32)
    hidden = (activate(first_pre) * inside[:, None, None, None]).astype(jnp.bfloat16)
    pre_mid = conv_depth(hidden, mid_kernel)
    pooled = pool_cells(activate(pre_mid)).astype(jnp.bfloat16)
    pre_deep = conv_depth(padded_2(pooled, (("space", 0),), 1), deep_kernel)
    pooled, pre_deep = lax.optimization_barrier((pooled, pre_deep))
    cotangent = deep_cotangent[0].astype(jnp.float32)
    grad_pre = (cotangent * activate_slope(pre_deep)).astype(jnp.bfloat16)
    flipped = jnp.swapaxes(deep_kernel[::-1, ::-1, ::-1], 3, 4)
    pooled_grad = conv_depth(padded_2(grad_pre, (("space", 0),), 1), flipped).astype(jnp.bfloat16)
    grad_pre, pooled_grad, pooled = lax.optimization_barrier((grad_pre, pooled_grad, pooled))
    columns = gather_columns(pooled, "space")
    all_grad_pre = gather_depth(grad_pre, "space")
    grad_mid = (expand(pooled_grad.astype(jnp.float32)) * 0.125 * activate_slope(pre_mid)).astype(
        jnp.bfloat16
    )
    mid_term = kernel_grad(pad_sides(hidden), grad_mid)
    mid_shape = mid_term.shape
    mid_grad, (columns, all_grad_pre) = reduce_all(
        mid_term.reshape(-1, mid_shape[-1]), ("dp", "space"), jnp.float32, (columns, all_grad_pre)
    )
    mid_grad = mid_grad.reshape(mid_shape)
    deep_term = kernel_grad(pad_cells(columns), all_grad_pre)
    deep_shape = deep_term.shape
    deep_grad, _ = reduce_all(deep_term.reshape(-1, deep_shape[-1]), ("dp",), jnp.bfloat16)
    deep_grad = deep_grad.reshape(deep_shape)
    device_total = lax.axis_size("dp") * space_count
    cell_count = slab_depth * side_cells * side_cells
    deep_scale = math.sqrt(device_total * cell_count // 8)
    mid_scale = math.sqrt(device_total * cell_count)
    deep_output = activate(pre_deep).astype(jnp.bfloat16)[None]
    return (deep_output, deep_grad / deep_scale, mid_grad / mid_scale)


def solution(mesh):
    in_specs = (P("dp", "space", None, None), P(), P(), P(), P("dp", "space", None, None, None))
    out_specs = (P("dp", "space", None, None, None), P(None, None, None, "space", None), P())
    return jax.shard_map(
        on_device, mesh=mesh, in_specs=in_specs, out_specs=out_specs, check_vma=False
    )
```

```python
import math

import jax
import jax.numpy as jnp
from jax import lax
from jax.sharding import PartitionSpec as P

SLOPE = 0.3


def padded_2(block, sides, width):
    for axis, dim in sides:
        count = lax.axis_size(axis)
        forward = [(i, i + 1) for i in range(count - 1)]
        backward = [(target, source) for source, target in forward]
        low = lax.ppermute(
            lax.slice_in_dim(block, block.shape[dim] - width, None, axis=dim), axis, forward
        )
        high = lax.ppermute(lax.slice_in_dim(block, 0, width, axis=dim), axis, backward)
        block = jnp.concatenate([low, block, high], axis=dim)
    return block


def digit_groups(axes):
    groups = []
    for axis in axes:
        bits = lax.axis_size(axis).bit_length() - 1
        bit = 1
        if bits % 2 == 1:
            groups.append((axis, 1, 2))
            bit = 2
        while bit < lax.axis_size(axis):
            groups.append((axis, bit, 4))
            bit *= 4
    return groups


def xor_pairs(axis, flip):
    return [(i, i ^ flip) for i in range(lax.axis_size(axis))]


def exchange_parts(block, axis, bit, radix):
    digit = (lax.axis_index(axis) // bit) % radix
    size = block.shape[0]
    out = jnp.zeros((radix * size,) + block.shape[1:], block.dtype)
    out = lax.dynamic_update_slice_in_dim(out, block, digit * size, 0)
    for t in range(1, radix):
        got = lax.ppermute(block, axis, xor_pairs(axis, t * bit))
        out = lax.dynamic_update_slice_in_dim(out, got, (digit ^ t) * size, 0)
    return out


def gather_depth(block, axis):
    for _, bit, radix in digit_groups((axis,)):
        block = exchange_parts(block, axis, bit, radix)
    return block


def gather_for_kernel_grad(pooled, grad_pre, axis):
    count = lax.axis_size(axis)
    me = lax.axis_index(axis)
    width = pooled.shape[3] // count
    slab = pooled.shape[0]
    both = (count * slab,) + pooled.shape[1:3]
    columns = jnp.zeros(both + (width,), pooled.dtype)
    full = jnp.zeros(both + grad_pre.shape[3:], grad_pre.dtype)
    own = lax.dynamic_slice_in_dim(pooled, me * width, width, 3)
    columns = lax.dynamic_update_slice_in_dim(columns, own, me * slab, 0)
    full = lax.dynamic_update_slice_in_dim(full, grad_pre, me * slab, 0)
    for t in range(1, count):
        part = lax.dynamic_slice_in_dim(pooled, (me ^ t) * width, width, 3)
        got = lax.ppermute(jnp.concatenate([part, grad_pre], 3), axis, xor_pairs(axis, t))
        columns = lax.dynamic_update_slice_in_dim(columns, got[..., :width], (me ^ t) * slab, 0)
        full = lax.dynamic_update_slice_in_dim(full, got[..., width:], (me ^ t) * slab, 0)
    return columns, full


def reduce_all(rows, axes, wire_dtype, tied=()):
    groups = digit_groups(axes)
    count = rows.shape[0]
    parts = 1
    for _, _, radix in groups:
        parts *= radix
    held = jnp.pad(rows, ((0, -count % parts), (0, 0)))
    for step, (axis, bit, radix) in enumerate(groups):
        digit = (lax.axis_index(axis) // bit) % radix
        size = held.shape[0] // radix
        total = lax.dynamic_slice_in_dim(held, digit * size, size, 0)
        for t in range(1, radix):
            send = lax.dynamic_slice_in_dim(held, (digit ^ t) * size, size, 0)
            got = lax.ppermute(send.astype(wire_dtype), axis, xor_pairs(axis, t * bit))
            total = total + got.astype(held.dtype)
        held = total
        if step == 0:
            held, tied = lax.optimization_barrier((held, tied))
    held = held.astype(wire_dtype)
    for axis, bit, radix in reversed(groups):
        held = exchange_parts(held, axis, bit, radix)
    return held[:count].astype(rows.dtype), tied


def activate(value):
    return SLOPE * value + (1.0 - SLOPE) * value * jax.nn.sigmoid(value)


def activate_slope(value):
    sig = jax.nn.sigmoid(value)
    return SLOPE + (1.0 - SLOPE) * (sig + value * sig * (1.0 - sig))


def conv_depth(padded, kernel):
    return lax.conv_general_dilated(
        padded[None],
        kernel,
        (1, 1, 1),
        [(0, 0), (1, 1), (1, 1)],
        dimension_numbers=("NDHWC", "DHWIO", "NDHWC"),
        preferred_element_type=jnp.float32,
    )[0]


def pool_cells(values):
    dd, hh, ww, cc = values.shape
    return values.reshape(dd // 2, 2, hh // 2, 2, ww // 2, 2, cc).mean(axis=(1, 3, 5))


def expand(values):
    return jnp.repeat(jnp.repeat(jnp.repeat(values, 2, 0), 2, 1), 2, 2)


def kernel_grad(padded, cotangent):
    dd, hh, ww, _ = cotangent.shape
    tap_list = []
    for depth_off in range(3):
        for row_off in range(3):
            for col_off in range(3):
                window = padded[
                    depth_off : depth_off + dd, row_off : row_off + hh, col_off : col_off + ww
                ]
                tap_list.append(
                    jnp.einsum(
                        "dhwi,dhwo->io", window, cotangent, preferred_element_type=jnp.float32
                    )
                )
    return jnp.stack(tap_list).reshape(3, 3, 3, padded.shape[-1], cotangent.shape[-1])


def pad_sides(values):
    return jnp.pad(values, ((0, 0), (1, 1), (1, 1), (0, 0)))


def pad_depth(values):
    return jnp.pad(values, ((1, 1), (0, 0), (0, 0), (0, 0)))


def pad_cells(values):
    return jnp.pad(values, ((1, 1), (1, 1), (1, 1), (0, 0)))


def on_device(volume, first_kernel, mid_kernel, deep_kernel, deep_cotangent):
    slab_depth = volume.shape[1]
    side_cells = volume.shape[2]
    in_channels = volume.shape[3] // side_cells
    space_count = lax.axis_size("space")
    space_index = lax.axis_index("space")
    input_field = volume[0].reshape(slab_depth, side_cells, side_cells, in_channels)
    padded = padded_2(input_field, (("space", 0),), 2)
    first_pre = conv_depth(padded, first_kernel)
    plane = space_index * slab_depth - 1 + jnp.arange(first_pre.shape[0])
    inside = ((plane >= 0) & (plane < space_count * slab_depth)).astype(jnp.float32)
    hidden = (activate(first_pre) * inside[:, None, None, None]).astype(jnp.bfloat16)
    pre_mid = conv_depth(hidden, mid_kernel)
    pooled = pool_cells(activate(pre_mid)).astype(jnp.bfloat16)
    pre_deep = conv_depth(padded_2(pooled, (("space", 0),), 1), deep_kernel)
    pooled, pre_deep = lax.optimization_barrier((pooled, pre_deep))
    cotangent = deep_cotangent[0].astype(jnp.float32)
    grad_pre = (cotangent * activate_slope(pre_deep)).astype(jnp.bfloat16)
    flipped = jnp.swapaxes(deep_kernel[::-1, ::-1, ::-1], 3, 4)
    pooled_grad = conv_depth(padded_2(grad_pre, (("space", 0),), 1), flipped).astype(jnp.bfloat16)
    grad_pre, pooled_grad, pooled = lax.optimization_barrier((grad_pre, pooled_grad, pooled))
    columns, all_grad_pre = gather_for_kernel_grad(pooled, grad_pre, "space")
    grad_mid = (expand(pooled_grad.astype(jnp.float32)) * 0.125 * activate_slope(pre_mid)).astype(
        jnp.bfloat16
    )
    mid_term = kernel_grad(pad_sides(hidden), grad_mid)
    mid_shape = mid_term.shape
    mid_grad, (columns, all_grad_pre) = reduce_all(
        mid_term.reshape(-1, mid_shape[-1]), ("dp", "space"), jnp.float32, (columns, all_grad_pre)
    )
    mid_grad = mid_grad.reshape(mid_shape)
    deep_term = kernel_grad(pad_cells(columns), all_grad_pre)
    deep_shape = deep_term.shape
    deep_grad, _ = reduce_all(deep_term.reshape(-1, deep_shape[-1]), ("dp",), jnp.bfloat16)
    deep_grad = deep_grad.reshape(deep_shape)
    device_total = lax.axis_size("dp") * space_count
    cell_count = slab_depth * side_cells * side_cells
    deep_scale = math.sqrt(device_total * cell_count // 8)
    mid_scale = math.sqrt(device_total * cell_count)
    deep_output = activate(pre_deep).astype(jnp.bfloat16)[None]
    return (deep_output, deep_grad / deep_scale, mid_grad / mid_scale)


def solution(mesh):
    in_specs = (P("dp", "space", None, None), P(), P(), P(), P("dp", "space", None, None, None))
    out_specs = (P("dp", "space", None, None, None), P(None, None, None, "space", None), P())
    return jax.shard_map(
        on_device, mesh=mesh, in_specs=in_specs, out_specs=out_specs, check_vma=False
    )
```

```python
import math

import jax
import jax.numpy as jnp
from jax import lax
from jax.sharding import PartitionSpec as P

SLOPE = 0.3


def padded_2(block, sides, width):
    for axis, dim in sides:
        count = lax.axis_size(axis)
        forward = [(i, i + 1) for i in range(count - 1)]
        backward = [(target, source) for source, target in forward]
        low = lax.ppermute(
            lax.slice_in_dim(block, block.shape[dim] - width, None, axis=dim), axis, forward
        )
        high = lax.ppermute(lax.slice_in_dim(block, 0, width, axis=dim), axis, backward)
        block = jnp.concatenate([low, block, high], axis=dim)
    return block


def digit_groups(axes):
    groups = []
    for axis in axes:
        bits = lax.axis_size(axis).bit_length() - 1
        bit = 1
        if bits % 2 == 1:
            groups.append((axis, 1, 2))
            bit = 2
        while bit < lax.axis_size(axis):
            groups.append((axis, bit, 4))
            bit *= 4
    return groups


def xor_pairs(axis, flip):
    return [(i, i ^ flip) for i in range(lax.axis_size(axis))]


def exchange_parts(block, axis, bit, radix):
    digit = (lax.axis_index(axis) // bit) % radix
    size = block.shape[0]
    out = jnp.zeros((radix * size,) + block.shape[1:], block.dtype)
    out = lax.dynamic_update_slice_in_dim(out, block, digit * size, 0)
    for t in range(1, radix):
        got = lax.ppermute(block, axis, xor_pairs(axis, t * bit))
        out = lax.dynamic_update_slice_in_dim(out, got, (digit ^ t) * size, 0)
    return out


def gather_depth(block, axis):
    for _, bit, radix in digit_groups((axis,)):
        block = exchange_parts(block, axis, bit, radix)
    return block


def gather_for_kernel_grad(pooled, grad_pre, axis):
    count = lax.axis_size(axis)
    me = lax.axis_index(axis)
    width = pooled.shape[3] // count
    slab = pooled.shape[0]
    both = (count * slab,) + pooled.shape[1:3]
    columns = jnp.zeros(both + (width,), pooled.dtype)
    full = jnp.zeros(both + grad_pre.shape[3:], grad_pre.dtype)
    own = lax.dynamic_slice_in_dim(pooled, me * width, width, 3)
    columns = lax.dynamic_update_slice_in_dim(columns, own, me * slab, 0)
    full = lax.dynamic_update_slice_in_dim(full, grad_pre, me * slab, 0)
    for t in range(1, count):
        part = lax.dynamic_slice_in_dim(pooled, (me ^ t) * width, width, 3)
        got = lax.ppermute(jnp.concatenate([part, grad_pre], 3), axis, xor_pairs(axis, t))
        columns = lax.dynamic_update_slice_in_dim(columns, got[..., :width], (me ^ t) * slab, 0)
        full = lax.dynamic_update_slice_in_dim(full, got[..., width:], (me ^ t) * slab, 0)
    return columns, full


def reduce_all(rows, axes, wire_dtype, tied=()):
    groups = digit_groups(axes)
    count = rows.shape[0]
    parts = 1
    for _, _, radix in groups:
        parts *= radix
    held = jnp.pad(rows, ((0, -count % parts), (0, 0)))
    for step, (axis, bit, radix) in enumerate(groups):
        digit = (lax.axis_index(axis) // bit) % radix
        size = held.shape[0] // radix
        total = lax.dynamic_slice_in_dim(held, digit * size, size, 0)
        for t in range(1, radix):
            send = lax.dynamic_slice_in_dim(held, (digit ^ t) * size, size, 0)
            got = lax.ppermute(send.astype(wire_dtype), axis, xor_pairs(axis, t * bit))
            total = total + got.astype(held.dtype)
        held = total
        if step == 0:
            held, tied = lax.optimization_barrier((held, tied))
    held = held.astype(wire_dtype)
    for axis, bit, radix in reversed(groups):
        held = exchange_parts(held, axis, bit, radix)
    return held[:count].astype(rows.dtype), tied


def activate(value):
    return SLOPE * value + (1.0 - SLOPE) * value * jax.nn.sigmoid(value)


def activate_slope(value):
    sig = jax.nn.sigmoid(value)
    return SLOPE + (1.0 - SLOPE) * (sig + value * sig * (1.0 - sig))


def conv_depth(padded, kernel):
    return lax.conv_general_dilated(
        padded[None],
        kernel,
        (1, 1, 1),
        [(0, 0), (1, 1), (1, 1)],
        dimension_numbers=("NDHWC", "DHWIO", "NDHWC"),
        preferred_element_type=jnp.float32,
    )[0]


def pool_cells(values):
    dd, hh, ww, cc = values.shape
    return values.reshape(dd // 2, 2, hh // 2, 2, ww // 2, 2, cc).mean(axis=(1, 3, 5))


def expand(values):
    return jnp.repeat(jnp.repeat(jnp.repeat(values, 2, 0), 2, 1), 2, 2)


def kernel_grad(padded, cotangent):
    dd, hh, ww, _ = cotangent.shape
    tap_list = []
    for depth_off in range(3):
        for row_off in range(3):
            for col_off in range(3):
                window = padded[
                    depth_off : depth_off + dd, row_off : row_off + hh, col_off : col_off + ww
                ]
                tap_list.append(
                    jnp.einsum(
                        "dhwi,dhwo->io", window, cotangent, preferred_element_type=jnp.float32
                    )
                )
    return jnp.stack(tap_list).reshape(3, 3, 3, padded.shape[-1], cotangent.shape[-1])


def pad_sides(values):
    return jnp.pad(values, ((0, 0), (1, 1), (1, 1), (0, 0)))


def pad_depth(values):
    return jnp.pad(values, ((1, 1), (0, 0), (0, 0), (0, 0)))


def pad_cells(values):
    return jnp.pad(values, ((1, 1), (1, 1), (1, 1), (0, 0)))


def on_device(volume, first_kernel, mid_kernel, deep_kernel, deep_cotangent):
    slab_depth = volume.shape[1]
    side_cells = volume.shape[2]
    in_channels = volume.shape[3] // side_cells
    space_count = lax.axis_size("space")
    space_index = lax.axis_index("space")
    input_field = volume[0].reshape(slab_depth, side_cells, side_cells, in_channels)
    padded = padded_2(input_field, (("space", 0),), 2)
    first_pre = conv_depth(padded, first_kernel)
    hidden = activate(first_pre).astype(jnp.bfloat16)
    low_keep = (space_index > 0).astype(hidden.dtype)
    high_keep = (space_index < space_count - 1).astype(hidden.dtype)
    hidden = lax.dynamic_update_slice_in_dim(hidden, hidden[:1] * low_keep, 0, 0)
    last = hidden.shape[0] - 1
    hidden = lax.dynamic_update_slice_in_dim(hidden, hidden[last:] * high_keep, last, 0)
    pre_mid = conv_depth(hidden, mid_kernel)
    pooled = pool_cells(activate(pre_mid)).astype(jnp.bfloat16)
    pre_deep = conv_depth(padded_2(pooled, (("space", 0),), 1), deep_kernel)
    pooled, pre_deep = lax.optimization_barrier((pooled, pre_deep))
    cotangent = deep_cotangent[0].astype(jnp.float32)
    grad_pre = (cotangent * activate_slope(pre_deep)).astype(jnp.bfloat16)
    flipped = jnp.swapaxes(deep_kernel[::-1, ::-1, ::-1], 3, 4)
    pooled_grad = conv_depth(padded_2(grad_pre, (("space", 0),), 1), flipped).astype(jnp.bfloat16)
    grad_pre, pooled_grad, pooled = lax.optimization_barrier((grad_pre, pooled_grad, pooled))
    columns, all_grad_pre = gather_for_kernel_grad(pooled, grad_pre, "space")
    grad_mid = (expand(pooled_grad.astype(jnp.float32)) * 0.125 * activate_slope(pre_mid)).astype(
        jnp.bfloat16
    )
    mid_term = kernel_grad(pad_sides(hidden), grad_mid)
    mid_shape = mid_term.shape
    mid_grad, (columns, all_grad_pre) = reduce_all(
        mid_term.reshape(-1, mid_shape[-1]), ("dp", "space"), jnp.float32, (columns, all_grad_pre)
    )
    mid_grad = mid_grad.reshape(mid_shape)
    deep_term = kernel_grad(pad_cells(columns), all_grad_pre)
    deep_shape = deep_term.shape
    deep_grad, _ = reduce_all(deep_term.reshape(-1, deep_shape[-1]), ("dp",), jnp.bfloat16)
    deep_grad = deep_grad.reshape(deep_shape)
    device_total = lax.axis_size("dp") * space_count
    cell_count = slab_depth * side_cells * side_cells
    deep_scale = math.sqrt(device_total * cell_count // 8)
    mid_scale = math.sqrt(device_total * cell_count)
    deep_output = activate(pre_deep).astype(jnp.bfloat16)[None]
    return (deep_output, deep_grad / deep_scale, mid_grad / mid_scale)


def solution(mesh):
    in_specs = (P("dp", "space", None, None), P(), P(), P(), P("dp", "space", None, None, None))
    out_specs = (P("dp", "space", None, None, None), P(None, None, None, "space", None), P())
    return jax.shard_map(
        on_device, mesh=mesh, in_specs=in_specs, out_specs=out_specs, check_vma=False
    )
```

```python
import math

import jax
import jax.numpy as jnp
from jax import lax
from jax.sharding import PartitionSpec as P

SLOPE = 0.3


def padded_2(block, sides, width):
    for axis, dim in sides:
        count = lax.axis_size(axis)
        forward = [(i, i + 1) for i in range(count - 1)]
        backward = [(target, source) for source, target in forward]
        low = lax.ppermute(
            lax.slice_in_dim(block, block.shape[dim] - width, None, axis=dim), axis, forward
        )
        high = lax.ppermute(lax.slice_in_dim(block, 0, width, axis=dim), axis, backward)
        block = jnp.concatenate([low, block, high], axis=dim)
    return block


def digit_groups(axes):
    groups = []
    for axis in axes:
        bits = lax.axis_size(axis).bit_length() - 1
        bit = 1
        if bits % 2 == 1:
            groups.append((axis, 1, 2))
            bit = 2
        while bit < lax.axis_size(axis):
            groups.append((axis, bit, 4))
            bit *= 4
    return groups


def xor_pairs(axis, flip):
    return [(i, i ^ flip) for i in range(lax.axis_size(axis))]


def exchange_parts(block, axis, bit, radix):
    digit = (lax.axis_index(axis) // bit) % radix
    size = block.shape[0]
    out = jnp.zeros((radix * size,) + block.shape[1:], block.dtype)
    out = lax.dynamic_update_slice_in_dim(out, block, digit * size, 0)
    for t in range(1, radix):
        got = lax.ppermute(block, axis, xor_pairs(axis, t * bit))
        out = lax.dynamic_update_slice_in_dim(out, got, (digit ^ t) * size, 0)
    return out


def gather_depth(block, axis):
    for _, bit, radix in digit_groups((axis,)):
        block = exchange_parts(block, axis, bit, radix)
    return block


def gather_for_kernel_grad(pooled, grad_pre, axis):
    count = lax.axis_size(axis)
    me = lax.axis_index(axis)
    width = pooled.shape[3] // count
    slab = pooled.shape[0]
    both = (count * slab,) + pooled.shape[1:3]
    columns = jnp.zeros(both + (width,), pooled.dtype)
    full = jnp.zeros(both + grad_pre.shape[3:], grad_pre.dtype)
    own = lax.dynamic_slice_in_dim(pooled, me * width, width, 3)
    columns = lax.dynamic_update_slice_in_dim(columns, own, me * slab, 0)
    full = lax.dynamic_update_slice_in_dim(full, grad_pre, me * slab, 0)
    for t in range(1, count):
        part = lax.dynamic_slice_in_dim(pooled, (me ^ t) * width, width, 3)
        got = lax.ppermute(jnp.concatenate([part, grad_pre], 3), axis, xor_pairs(axis, t))
        columns = lax.dynamic_update_slice_in_dim(columns, got[..., :width], (me ^ t) * slab, 0)
        full = lax.dynamic_update_slice_in_dim(full, got[..., width:], (me ^ t) * slab, 0)
    return columns, full


def reduce_all(rows, axes, wire_dtype, tied=()):
    groups = digit_groups(axes)
    count = rows.shape[0]
    parts = 1
    for _, _, radix in groups:
        parts *= radix
    held = jnp.pad(rows, ((0, -count % parts), (0, 0)))
    for step, (axis, bit, radix) in enumerate(groups):
        digit = (lax.axis_index(axis) // bit) % radix
        size = held.shape[0] // radix
        total = lax.dynamic_slice_in_dim(held, digit * size, size, 0)
        for t in range(1, radix):
            send = lax.dynamic_slice_in_dim(held, (digit ^ t) * size, size, 0)
            got = lax.ppermute(send.astype(wire_dtype), axis, xor_pairs(axis, t * bit))
            total = total + got.astype(held.dtype)
        held = total
        if step == 0:
            held, tied = lax.optimization_barrier((held, tied))
    held = held.astype(wire_dtype)
    for axis, bit, radix in reversed(groups):
        held = exchange_parts(held, axis, bit, radix)
    return held[:count].astype(rows.dtype), tied


def activate(value):
    return SLOPE * value + (1.0 - SLOPE) * value * jax.nn.sigmoid(value)


def activate_slope(value):
    sig = jax.nn.sigmoid(value)
    return SLOPE + (1.0 - SLOPE) * (sig + value * sig * (1.0 - sig))


def conv_depth(padded, kernel):
    return lax.conv_general_dilated(
        padded[None],
        kernel,
        (1, 1, 1),
        [(0, 0), (1, 1), (1, 1)],
        dimension_numbers=("NDHWC", "DHWIO", "NDHWC"),
        preferred_element_type=jnp.float32,
    )[0]


def pool_cells(values):
    dd, hh, ww, cc = values.shape
    return values.reshape(dd // 2, 2, hh // 2, 2, ww // 2, 2, cc).mean(axis=(1, 3, 5))


def expand(values):
    return jnp.repeat(jnp.repeat(jnp.repeat(values, 2, 0), 2, 1), 2, 2)


def kernel_grad(padded, cotangent):
    dd, hh, ww, _ = cotangent.shape
    chans = padded.shape[-1]

    def tap(index, total):
        start = (index // 9, (index // 3) % 3, index % 3, 0)
        window = lax.dynamic_slice(padded, start, (dd, hh, ww, chans))
        term = jnp.einsum("dhwi,dhwo->io", window, cotangent, preferred_element_type=jnp.float32)
        return lax.dynamic_update_index_in_dim(total, term, index, 0)

    total = jnp.zeros((27, chans, cotangent.shape[-1]), jnp.float32)
    total = lax.fori_loop(0, 27, tap, total)
    return total.reshape(3, 3, 3, chans, cotangent.shape[-1])


def pad_sides(values):
    return jnp.pad(values, ((0, 0), (1, 1), (1, 1), (0, 0)))


def pad_depth(values):
    return jnp.pad(values, ((1, 1), (0, 0), (0, 0), (0, 0)))


def pad_cells(values):
    return jnp.pad(values, ((1, 1), (1, 1), (1, 1), (0, 0)))


def on_device(volume, first_kernel, mid_kernel, deep_kernel, deep_cotangent):
    slab_depth = volume.shape[1]
    side_cells = volume.shape[2]
    in_channels = volume.shape[3] // side_cells
    space_count = lax.axis_size("space")
    space_index = lax.axis_index("space")
    input_field = volume[0].reshape(slab_depth, side_cells, side_cells, in_channels)
    padded = padded_2(input_field, (("space", 0),), 2)
    first_pre = conv_depth(padded, first_kernel)
    plane = space_index * slab_depth - 1 + jnp.arange(first_pre.shape[0])
    inside = ((plane >= 0) & (plane < space_count * slab_depth)).astype(jnp.float32)
    hidden = (activate(first_pre) * inside[:, None, None, None]).astype(jnp.bfloat16)
    pre_mid = conv_depth(hidden, mid_kernel)
    pooled = pool_cells(activate(pre_mid)).astype(jnp.bfloat16)
    pre_deep = conv_depth(padded_2(pooled, (("space", 0),), 1), deep_kernel)
    pooled, pre_deep = lax.optimization_barrier((pooled, pre_deep))
    cotangent = deep_cotangent[0].astype(jnp.float32)
    grad_pre = (cotangent * activate_slope(pre_deep)).astype(jnp.bfloat16)
    flipped = jnp.swapaxes(deep_kernel[::-1, ::-1, ::-1], 3, 4)
    pooled_grad = conv_depth(padded_2(grad_pre, (("space", 0),), 1), flipped).astype(jnp.bfloat16)
    grad_pre, pooled_grad, pooled = lax.optimization_barrier((grad_pre, pooled_grad, pooled))
    columns, all_grad_pre = gather_for_kernel_grad(pooled, grad_pre, "space")
    grad_mid = (expand(pooled_grad.astype(jnp.float32)) * 0.125 * activate_slope(pre_mid)).astype(
        jnp.bfloat16
    )
    mid_term = kernel_grad(pad_sides(hidden), grad_mid)
    mid_shape = mid_term.shape
    mid_grad, (columns, all_grad_pre) = reduce_all(
        mid_term.reshape(-1, mid_shape[-1]), ("dp", "space"), jnp.float32, (columns, all_grad_pre)
    )
    mid_grad = mid_grad.reshape(mid_shape)
    deep_term = kernel_grad(pad_cells(columns), all_grad_pre)
    deep_shape = deep_term.shape
    deep_grad, _ = reduce_all(deep_term.reshape(-1, deep_shape[-1]), ("dp",), jnp.bfloat16)
    deep_grad = deep_grad.reshape(deep_shape)
    device_total = lax.axis_size("dp") * space_count
    cell_count = slab_depth * side_cells * side_cells
    deep_scale = math.sqrt(device_total * cell_count // 8)
    mid_scale = math.sqrt(device_total * cell_count)
    deep_output = activate(pre_deep).astype(jnp.bfloat16)[None]
    return (deep_output, deep_grad / deep_scale, mid_grad / mid_scale)


def solution(mesh):
    in_specs = (P("dp", "space", None, None), P(), P(), P(), P("dp", "space", None, None, None))
    out_specs = (P("dp", "space", None, None, None), P(None, None, None, "space", None), P())
    return jax.shard_map(
        on_device, mesh=mesh, in_specs=in_specs, out_specs=out_specs, check_vma=False
    )
```

```python
import math

import jax
import jax.numpy as jnp
from jax import lax
from jax.sharding import PartitionSpec as P

SLOPE = 0.3


def padded_2(block, sides, width):
    for axis, dim in sides:
        count = lax.axis_size(axis)
        forward = [(i, i + 1) for i in range(count - 1)]
        backward = [(target, source) for source, target in forward]
        low = lax.ppermute(
            lax.slice_in_dim(block, block.shape[dim] - width, None, axis=dim), axis, forward
        )
        high = lax.ppermute(lax.slice_in_dim(block, 0, width, axis=dim), axis, backward)
        block = jnp.concatenate([low, block, high], axis=dim)
    return block


def digit_groups(axes):
    groups = []
    for axis in axes:
        bits = lax.axis_size(axis).bit_length() - 1
        bit = 1
        if bits % 2 == 1:
            groups.append((axis, 1, 2))
            bit = 2
        while bit < lax.axis_size(axis):
            groups.append((axis, bit, 4))
            bit *= 4
    return groups


def xor_pairs(axis, flip):
    return [(i, i ^ flip) for i in range(lax.axis_size(axis))]


def exchange_parts(block, axis, bit, radix):
    digit = (lax.axis_index(axis) // bit) % radix
    size = block.shape[0]
    out = jnp.zeros((radix * size,) + block.shape[1:], block.dtype)
    out = lax.dynamic_update_slice_in_dim(out, block, digit * size, 0)
    for t in range(1, radix):
        got = lax.ppermute(block, axis, xor_pairs(axis, t * bit))
        out = lax.dynamic_update_slice_in_dim(out, got, (digit ^ t) * size, 0)
    return out


def gather_depth(block, axis):
    for _, bit, radix in digit_groups((axis,)):
        block = exchange_parts(block, axis, bit, radix)
    return block


def gather_for_kernel_grad(pooled, grad_pre, axis):
    count = lax.axis_size(axis)
    me = lax.axis_index(axis)
    width = pooled.shape[3] // count
    slab = pooled.shape[0]
    both = (count * slab,) + pooled.shape[1:3]
    columns = jnp.zeros(both + (width,), pooled.dtype)
    full = jnp.zeros(both + grad_pre.shape[3:], grad_pre.dtype)
    own = lax.dynamic_slice_in_dim(pooled, me * width, width, 3)
    columns = lax.dynamic_update_slice_in_dim(columns, own, me * slab, 0)
    full = lax.dynamic_update_slice_in_dim(full, grad_pre, me * slab, 0)
    for t in range(1, count):
        part = lax.dynamic_slice_in_dim(pooled, (me ^ t) * width, width, 3)
        got = lax.ppermute(jnp.concatenate([part, grad_pre], 3), axis, xor_pairs(axis, t))
        columns = lax.dynamic_update_slice_in_dim(columns, got[..., :width], (me ^ t) * slab, 0)
        full = lax.dynamic_update_slice_in_dim(full, got[..., width:], (me ^ t) * slab, 0)
    return columns, full


def reduce_all(rows, axes, wire_dtype, tied=()):
    groups = digit_groups(axes)
    count = rows.shape[0]
    parts = 1
    for _, _, radix in groups:
        parts *= radix
    held = jnp.pad(rows, ((0, -count % parts), (0, 0)))
    for step, (axis, bit, radix) in enumerate(groups):
        digit = (lax.axis_index(axis) // bit) % radix
        size = held.shape[0] // radix
        total = lax.dynamic_slice_in_dim(held, digit * size, size, 0)
        for t in range(1, radix):
            send = lax.dynamic_slice_in_dim(held, (digit ^ t) * size, size, 0)
            got = lax.ppermute(send.astype(wire_dtype), axis, xor_pairs(axis, t * bit))
            total = total + got.astype(held.dtype)
        held = total
        if step < len(tied):
            held, ready = lax.optimization_barrier((held, tied[step]))
            tied = tied[:step] + (ready,) + tied[step + 1 :]
    held = held.astype(wire_dtype)
    for axis, bit, radix in reversed(groups):
        held = exchange_parts(held, axis, bit, radix)
    return held[:count].astype(rows.dtype), tied


def activate(value):
    return SLOPE * value + (1.0 - SLOPE) * value * jax.nn.sigmoid(value)


def activate_slope(value):
    sig = jax.nn.sigmoid(value)
    return SLOPE + (1.0 - SLOPE) * (sig + value * sig * (1.0 - sig))


def conv_depth(padded, kernel):
    return lax.conv_general_dilated(
        padded[None],
        kernel,
        (1, 1, 1),
        [(0, 0), (1, 1), (1, 1)],
        dimension_numbers=("NDHWC", "DHWIO", "NDHWC"),
        preferred_element_type=jnp.float32,
    )[0]


def pool_cells(values):
    dd, hh, ww, cc = values.shape
    return values.reshape(dd // 2, 2, hh // 2, 2, ww // 2, 2, cc).mean(axis=(1, 3, 5))


def expand(values):
    return jnp.repeat(jnp.repeat(jnp.repeat(values, 2, 0), 2, 1), 2, 2)


def tap_terms(padded, cotangent, taps):
    dd, hh, ww, _ = cotangent.shape
    terms = []
    for tap in taps:
        depth_off, row_off, col_off = tap // 9, (tap // 3) % 3, tap % 3
        window = padded[
            depth_off : depth_off + dd, row_off : row_off + hh, col_off : col_off + ww
        ]
        terms.append(
            jnp.einsum("dhwi,dhwo->io", window, cotangent, preferred_element_type=jnp.float32)
        )
    return terms


def kernel_grad(padded, cotangent):
    terms = tap_terms(padded, cotangent, range(27))
    return jnp.stack(terms).reshape(3, 3, 3, padded.shape[-1], cotangent.shape[-1])


def pad_sides(values):
    return jnp.pad(values, ((0, 0), (1, 1), (1, 1), (0, 0)))


def pad_depth(values):
    return jnp.pad(values, ((1, 1), (0, 0), (0, 0), (0, 0)))


def pad_cells(values):
    return jnp.pad(values, ((1, 1), (1, 1), (1, 1), (0, 0)))


def on_device(volume, first_kernel, mid_kernel, deep_kernel, deep_cotangent):
    slab_depth = volume.shape[1]
    side_cells = volume.shape[2]
    in_channels = volume.shape[3] // side_cells
    space_count = lax.axis_size("space")
    space_index = lax.axis_index("space")
    input_field = volume[0].reshape(slab_depth, side_cells, side_cells, in_channels)
    padded = padded_2(input_field, (("space", 0),), 2)
    first_pre = conv_depth(padded, first_kernel)
    plane = space_index * slab_depth - 1 + jnp.arange(first_pre.shape[0])
    inside = ((plane >= 0) & (plane < space_count * slab_depth)).astype(jnp.float32)
    hidden = (activate(first_pre) * inside[:, None, None, None]).astype(jnp.bfloat16)
    pre_mid = conv_depth(hidden, mid_kernel)
    pooled = pool_cells(activate(pre_mid)).astype(jnp.bfloat16)
    pre_deep = conv_depth(padded_2(pooled, (("space", 0),), 1), deep_kernel)
    pooled, pre_deep = lax.optimization_barrier((pooled, pre_deep))
    cotangent = deep_cotangent[0].astype(jnp.float32)
    grad_pre = (cotangent * activate_slope(pre_deep)).astype(jnp.bfloat16)
    flipped = jnp.swapaxes(deep_kernel[::-1, ::-1, ::-1], 3, 4)
    pooled_grad = conv_depth(padded_2(grad_pre, (("space", 0),), 1), flipped).astype(jnp.bfloat16)
    grad_pre, pooled_grad, pooled = lax.optimization_barrier((grad_pre, pooled_grad, pooled))
    columns, all_grad_pre = gather_for_kernel_grad(pooled, grad_pre, "space")
    grad_mid = (expand(pooled_grad.astype(jnp.float32)) * 0.125 * activate_slope(pre_mid)).astype(
        jnp.bfloat16
    )
    mid_term = kernel_grad(pad_sides(hidden), grad_mid)
    mid_shape = mid_term.shape
    inputs = (columns, all_grad_pre)
    mid_grad, (early, late) = reduce_all(
        mid_term.reshape(-1, mid_shape[-1]), ("dp", "space"), jnp.float32, (inputs, inputs)
    )
    mid_grad = mid_grad.reshape(mid_shape)
    terms = tap_terms(pad_cells(early[0]), early[1], range(14))
    terms += tap_terms(pad_cells(late[0]), late[1], range(14, 27))
    deep_term = jnp.stack(terms).reshape(3, 3, 3, columns.shape[-1], all_grad_pre.shape[-1])
    deep_shape = deep_term.shape
    deep_grad, _ = reduce_all(deep_term.reshape(-1, deep_shape[-1]), ("dp",), jnp.bfloat16)
    deep_grad = deep_grad.reshape(deep_shape)
    device_total = lax.axis_size("dp") * space_count
    cell_count = slab_depth * side_cells * side_cells
    deep_scale = math.sqrt(device_total * cell_count // 8)
    mid_scale = math.sqrt(device_total * cell_count)
    deep_output = activate(pre_deep).astype(jnp.bfloat16)[None]
    return (deep_output, deep_grad / deep_scale, mid_grad / mid_scale)


def solution(mesh):
    in_specs = (P("dp", "space", None, None), P(), P(), P(), P("dp", "space", None, None, None))
    out_specs = (P("dp", "space", None, None, None), P(None, None, None, "space", None), P())
    return jax.shard_map(
        on_device, mesh=mesh, in_specs=in_specs, out_specs=out_specs, check_vma=False
    )
```

```python
import math

import jax
import jax.numpy as jnp
from jax import lax
from jax.sharding import PartitionSpec as P

SLOPE = 0.3


def padded_2(block, sides, width):
    for axis, dim in sides:
        count = lax.axis_size(axis)
        forward = [(i, i + 1) for i in range(count - 1)]
        backward = [(target, source) for source, target in forward]
        low = lax.ppermute(
            lax.slice_in_dim(block, block.shape[dim] - width, None, axis=dim), axis, forward
        )
        high = lax.ppermute(lax.slice_in_dim(block, 0, width, axis=dim), axis, backward)
        block = jnp.concatenate([low, block, high], axis=dim)
    return block


def digit_groups(axes):
    groups = []
    for axis in axes:
        bits = lax.axis_size(axis).bit_length() - 1
        bit = 1
        if bits % 2 == 1:
            groups.append((axis, 1, 2))
            bit = 2
        while bit < lax.axis_size(axis):
            groups.append((axis, bit, 4))
            bit *= 4
    return groups


def xor_pairs(axis, flip):
    return [(i, i ^ flip) for i in range(lax.axis_size(axis))]


def exchange_parts(block, axis, bit, radix):
    digit = (lax.axis_index(axis) // bit) % radix
    size = block.shape[0]
    out = jnp.zeros((radix * size,) + block.shape[1:], block.dtype)
    out = lax.dynamic_update_slice_in_dim(out, block, digit * size, 0)
    for t in range(1, radix):
        got = lax.ppermute(block, axis, xor_pairs(axis, t * bit))
        out = lax.dynamic_update_slice_in_dim(out, got, (digit ^ t) * size, 0)
    return out


def gather_depth(block, axis):
    for _, bit, radix in digit_groups((axis,)):
        block = exchange_parts(block, axis, bit, radix)
    return block


def reduce_all(rows, axes, wire_dtype, tied=()):
    groups = digit_groups(axes)
    count = rows.shape[0]
    parts = 1
    for _, _, radix in groups:
        parts *= radix
    held = jnp.pad(rows, ((0, -count % parts), (0, 0)))
    for step, (axis, bit, radix) in enumerate(groups):
        digit = (lax.axis_index(axis) // bit) % radix
        size = held.shape[0] // radix
        total = lax.dynamic_slice_in_dim(held, digit * size, size, 0)
        for t in range(1, radix):
            send = lax.dynamic_slice_in_dim(held, (digit ^ t) * size, size, 0)
            got = lax.ppermute(send.astype(wire_dtype), axis, xor_pairs(axis, t * bit))
            total = total + got.astype(held.dtype)
        held = total
        if step < len(tied):
            held, ready = lax.optimization_barrier((held, tied[step]))
            tied = tied[:step] + (ready,) + tied[step + 1 :]
    held = held.astype(wire_dtype)
    for axis, bit, radix in reversed(groups):
        held = exchange_parts(held, axis, bit, radix)
    return held[:count].astype(rows.dtype), tied


def activate(value):
    return SLOPE * value + (1.0 - SLOPE) * value * jax.nn.sigmoid(value)


def activate_slope(value):
    sig = jax.nn.sigmoid(value)
    return SLOPE + (1.0 - SLOPE) * (sig + value * sig * (1.0 - sig))


def conv_depth(padded, kernel):
    return lax.conv_general_dilated(
        padded[None],
        kernel,
        (1, 1, 1),
        [(0, 0), (1, 1), (1, 1)],
        dimension_numbers=("NDHWC", "DHWIO", "NDHWC"),
        preferred_element_type=jnp.float32,
    )[0]


def pool_cells(values):
    dd, hh, ww, cc = values.shape
    return values.reshape(dd // 2, 2, hh // 2, 2, ww // 2, 2, cc).mean(axis=(1, 3, 5))


def expand(values):
    return jnp.repeat(jnp.repeat(jnp.repeat(values, 2, 0), 2, 1), 2, 2)


def tap_terms(padded, cotangent, taps):
    dd, hh, ww, _ = cotangent.shape
    terms = []
    for tap in taps:
        depth_off, row_off, col_off = tap // 9, (tap // 3) % 3, tap % 3
        window = padded[
            depth_off : depth_off + dd, row_off : row_off + hh, col_off : col_off + ww
        ]
        terms.append(
            jnp.einsum("dhwi,dhwo->io", window, cotangent, preferred_element_type=jnp.float32)
        )
    return terms


def kernel_grad(padded, cotangent):
    terms = tap_terms(padded, cotangent, range(27))
    return jnp.stack(terms).reshape(3, 3, 3, padded.shape[-1], cotangent.shape[-1])


def pad_sides(values):
    return jnp.pad(values, ((0, 0), (1, 1), (1, 1), (0, 0)))


def pad_depth(values):
    return jnp.pad(values, ((1, 1), (0, 0), (0, 0), (0, 0)))


def pad_cells(values):
    return jnp.pad(values, ((1, 1), (1, 1), (1, 1), (0, 0)))


def on_device(volume, first_kernel, mid_kernel, deep_kernel, deep_cotangent):
    slab_depth = volume.shape[1]
    side_cells = volume.shape[2]
    in_channels = volume.shape[3] // side_cells
    space_count = lax.axis_size("space")
    space_index = lax.axis_index("space")
    input_field = volume[0].reshape(slab_depth, side_cells, side_cells, in_channels)
    padded = padded_2(input_field, (("space", 0),), 2)
    first_pre = conv_depth(padded, first_kernel)
    plane = space_index * slab_depth - 1 + jnp.arange(first_pre.shape[0])
    inside = ((plane >= 0) & (plane < space_count * slab_depth)).astype(jnp.float32)
    hidden = (activate(first_pre) * inside[:, None, None, None]).astype(jnp.bfloat16)
    pre_mid = conv_depth(hidden, mid_kernel)
    pooled = pool_cells(activate(pre_mid)).astype(jnp.bfloat16)
    pre_deep = conv_depth(padded_2(pooled, (("space", 0),), 1), deep_kernel)
    pooled, pre_deep = lax.optimization_barrier((pooled, pre_deep))
    cotangent = deep_cotangent[0].astype(jnp.float32)
    all_cotangent = gather_depth(deep_cotangent[0], "space")
    grad_pre = (cotangent * activate_slope(pre_deep)).astype(jnp.bfloat16)
    flipped = jnp.swapaxes(deep_kernel[::-1, ::-1, ::-1], 3, 4)
    pooled_grad = conv_depth(padded_2(grad_pre, (("space", 0),), 1), flipped).astype(jnp.bfloat16)
    grad_pre, pooled_grad, pooled = lax.optimization_barrier((grad_pre, pooled_grad, pooled))
    all_pooled = gather_depth(pooled, "space")
    all_pre_deep = conv_depth(pad_depth(all_pooled), deep_kernel)
    all_grad_pre = (all_cotangent.astype(jnp.float32) * activate_slope(all_pre_deep)).astype(
        jnp.bfloat16
    )
    chan_width = pooled.shape[3] // space_count
    columns = lax.dynamic_slice_in_dim(all_pooled, space_index * chan_width, chan_width, 3)
    grad_mid = (expand(pooled_grad.astype(jnp.float32)) * 0.125 * activate_slope(pre_mid)).astype(
        jnp.bfloat16
    )
    mid_term = kernel_grad(pad_sides(hidden), grad_mid)
    mid_shape = mid_term.shape
    inputs = (columns, all_grad_pre)
    mid_grad, (early, late) = reduce_all(
        mid_term.reshape(-1, mid_shape[-1]), ("dp", "space"), jnp.float32, (inputs, inputs)
    )
    mid_grad = mid_grad.reshape(mid_shape)
    terms = tap_terms(pad_cells(early[0]), early[1], range(14))
    terms += tap_terms(pad_cells(late[0]), late[1], range(14, 27))
    deep_term = jnp.stack(terms).reshape(3, 3, 3, columns.shape[-1], all_grad_pre.shape[-1])
    deep_shape = deep_term.shape
    deep_grad, _ = reduce_all(deep_term.reshape(-1, deep_shape[-1]), ("dp",), jnp.bfloat16)
    deep_grad = deep_grad.reshape(deep_shape)
    device_total = lax.axis_size("dp") * space_count
    cell_count = slab_depth * side_cells * side_cells
    deep_scale = math.sqrt(device_total * cell_count // 8)
    mid_scale = math.sqrt(device_total * cell_count)
    deep_output = activate(pre_deep).astype(jnp.bfloat16)[None]
    return (deep_output, deep_grad / deep_scale, mid_grad / mid_scale)


def solution(mesh):
    in_specs = (P("dp", "space", None, None), P(), P(), P(), P("dp", "space", None, None, None))
    out_specs = (P("dp", "space", None, None, None), P(None, None, None, "space", None), P())
    return jax.shard_map(
        on_device, mesh=mesh, in_specs=in_specs, out_specs=out_specs, check_vma=False
    )
```

```python
import math

import jax
import jax.numpy as jnp
from jax import lax
from jax.sharding import PartitionSpec as P

SLOPE = 0.3


def padded_2(block, sides, width):
    for axis, dim in sides:
        count = lax.axis_size(axis)
        forward = [(i, i + 1) for i in range(count - 1)]
        backward = [(target, source) for source, target in forward]
        low = lax.ppermute(
            lax.slice_in_dim(block, block.shape[dim] - width, None, axis=dim), axis, forward
        )
        high = lax.ppermute(lax.slice_in_dim(block, 0, width, axis=dim), axis, backward)
        block = jnp.concatenate([low, block, high], axis=dim)
    return block


def digit_groups(axes):
    groups = []
    for axis in axes:
        bits = lax.axis_size(axis).bit_length() - 1
        bit = 1
        if bits % 2 == 1:
            groups.append((axis, 1, 2))
            bit = 2
        while bit < lax.axis_size(axis):
            groups.append((axis, bit, 4))
            bit *= 4
    return groups


def xor_pairs(axis, flip):
    return [(i, i ^ flip) for i in range(lax.axis_size(axis))]


def exchange_parts(block, axis, bit, radix):
    digit = (lax.axis_index(axis) // bit) % radix
    size = block.shape[0]
    out = jnp.zeros((radix * size,) + block.shape[1:], block.dtype)
    out = lax.dynamic_update_slice_in_dim(out, block, digit * size, 0)
    for t in range(1, radix):
        got = lax.ppermute(block, axis, xor_pairs(axis, t * bit))
        out = lax.dynamic_update_slice_in_dim(out, got, (digit ^ t) * size, 0)
    return out


def gather_depth(block, axis):
    for _, bit, radix in digit_groups((axis,)):
        block = exchange_parts(block, axis, bit, radix)
    return block


def gather_for_kernel_grad(pooled, grad_pre, axis):
    count = lax.axis_size(axis)
    me = lax.axis_index(axis)
    width = pooled.shape[3] // count
    slab = pooled.shape[0]
    both = (count * slab,) + pooled.shape[1:3]
    columns = jnp.zeros(both + (width,), pooled.dtype)
    full = jnp.zeros(both + grad_pre.shape[3:], grad_pre.dtype)
    own = lax.dynamic_slice_in_dim(pooled, me * width, width, 3)
    columns = lax.dynamic_update_slice_in_dim(columns, own, me * slab, 0)
    full = lax.dynamic_update_slice_in_dim(full, grad_pre, me * slab, 0)
    for t in range(1, count):
        part = lax.dynamic_slice_in_dim(pooled, (me ^ t) * width, width, 3)
        got = lax.ppermute(jnp.concatenate([part, grad_pre], 3), axis, xor_pairs(axis, t))
        columns = lax.dynamic_update_slice_in_dim(columns, got[..., :width], (me ^ t) * slab, 0)
        full = lax.dynamic_update_slice_in_dim(full, got[..., width:], (me ^ t) * slab, 0)
    return columns, full


def reduce_all(rows, axes, wire_dtype, tied=()):
    groups = digit_groups(axes)
    count = rows.shape[0]
    parts = 1
    for _, _, radix in groups:
        parts *= radix
    held = jnp.pad(rows, ((0, -count % parts), (0, 0)))
    for step, (axis, bit, radix) in enumerate(groups):
        digit = (lax.axis_index(axis) // bit) % radix
        size = held.shape[0] // radix
        total = lax.dynamic_slice_in_dim(held, digit * size, size, 0)
        for t in range(1, radix):
            send = lax.dynamic_slice_in_dim(held, (digit ^ t) * size, size, 0)
            got = lax.ppermute(send.astype(wire_dtype), axis, xor_pairs(axis, t * bit))
            total = total + got.astype(held.dtype)
        held = total
        if step < len(tied):
            held, ready = lax.optimization_barrier((held, tied[step]))
            tied = tied[:step] + (ready,) + tied[step + 1 :]
    held = held.astype(wire_dtype)
    for axis, bit, radix in reversed(groups):
        held = exchange_parts(held, axis, bit, radix)
    return held[:count].astype(rows.dtype), tied


def activate(value):
    return SLOPE * value + (1.0 - SLOPE) * value * jax.nn.sigmoid(value)


def activate_slope(value):
    sig = jax.nn.sigmoid(value)
    return SLOPE + (1.0 - SLOPE) * (sig + value * sig * (1.0 - sig))


def conv_depth(padded, kernel):
    return lax.conv_general_dilated(
        padded[None],
        kernel,
        (1, 1, 1),
        [(0, 0), (1, 1), (1, 1)],
        dimension_numbers=("NDHWC", "DHWIO", "NDHWC"),
        preferred_element_type=jnp.float32,
    )[0]


def pool_cells(values):
    dd, hh, ww, cc = values.shape
    return values.reshape(dd // 2, 2, hh // 2, 2, ww // 2, 2, cc).mean(axis=(1, 3, 5))


def expand(values):
    return jnp.repeat(jnp.repeat(jnp.repeat(values, 2, 0), 2, 1), 2, 2)


def tap_terms(padded, cotangent, taps):
    dd, hh, ww, _ = cotangent.shape
    terms = []
    for tap in taps:
        depth_off, row_off, col_off = tap // 9, (tap // 3) % 3, tap % 3
        window = padded[
            depth_off : depth_off + dd, row_off : row_off + hh, col_off : col_off + ww
        ]
        terms.append(
            jnp.einsum("dhwi,dhwo->io", window, cotangent, preferred_element_type=jnp.float32)
        )
    return terms


def kernel_grad(padded, cotangent):
    terms = tap_terms(padded, cotangent, range(27))
    return jnp.stack(terms).reshape(3, 3, 3, padded.shape[-1], cotangent.shape[-1])


def pad_sides(values):
    return jnp.pad(values, ((0, 0), (1, 1), (1, 1), (0, 0)))


def pad_depth(values):
    return jnp.pad(values, ((1, 1), (0, 0), (0, 0), (0, 0)))


def pad_cells(values):
    return jnp.pad(values, ((1, 1), (1, 1), (1, 1), (0, 0)))


def on_device(volume, first_kernel, mid_kernel, deep_kernel, deep_cotangent):
    slab_depth = volume.shape[1]
    side_cells = volume.shape[2]
    in_channels = volume.shape[3] // side_cells
    space_count = lax.axis_size("space")
    space_index = lax.axis_index("space")
    input_field = volume[0].reshape(slab_depth, side_cells, side_cells, in_channels)
    padded = padded_2(input_field, (("space", 0),), 2)
    first_pre = conv_depth(padded, first_kernel)
    plane = space_index * slab_depth - 1 + jnp.arange(first_pre.shape[0])
    inside = ((plane >= 0) & (plane < space_count * slab_depth)).astype(jnp.float32)
    hidden = (activate(first_pre) * inside[:, None, None, None]).astype(jnp.bfloat16)
    pre_mid = conv_depth(hidden, mid_kernel)
    pooled = pool_cells(activate(pre_mid)).astype(jnp.bfloat16)
    pre_deep = conv_depth(padded_2(pooled, (("space", 0),), 1), deep_kernel)
    pooled, pre_deep = lax.optimization_barrier((pooled, pre_deep))
    cotangent = deep_cotangent[0].astype(jnp.float32)
    grad_pre = (cotangent * activate_slope(pre_deep)).astype(jnp.bfloat16)
    flipped = jnp.swapaxes(deep_kernel[::-1, ::-1, ::-1], 3, 4)
    pooled_grad = conv_depth(padded_2(grad_pre, (("space", 0),), 1), flipped).astype(jnp.bfloat16)
    grad_pre, pooled_grad, pooled = lax.optimization_barrier((grad_pre, pooled_grad, pooled))
    columns, all_grad_pre = gather_for_kernel_grad(pooled, grad_pre, "space")
    grad_mid = (expand(pooled_grad.astype(jnp.float32)) * 0.125 * activate_slope(pre_mid)).astype(
        jnp.bfloat16
    )
    mid_term = kernel_grad(pad_sides(hidden), grad_mid)
    mid_shape = mid_term.shape
    inputs = (columns, all_grad_pre)
    mid_grad, (_, early, late) = reduce_all(
        mid_term.reshape(-1, mid_shape[-1]), ("dp", "space"), jnp.float32, ((), inputs, inputs)
    )
    mid_grad = mid_grad.reshape(mid_shape)
    terms = tap_terms(pad_cells(early[0]), early[1], range(14))
    terms += tap_terms(pad_cells(late[0]), late[1], range(14, 27))
    deep_term = jnp.stack(terms).reshape(3, 3, 3, columns.shape[-1], all_grad_pre.shape[-1])
    deep_shape = deep_term.shape
    deep_grad, _ = reduce_all(deep_term.reshape(-1, deep_shape[-1]), ("dp",), jnp.bfloat16)
    deep_grad = deep_grad.reshape(deep_shape)
    device_total = lax.axis_size("dp") * space_count
    cell_count = slab_depth * side_cells * side_cells
    deep_scale = math.sqrt(device_total * cell_count // 8)
    mid_scale = math.sqrt(device_total * cell_count)
    deep_output = activate(pre_deep).astype(jnp.bfloat16)[None]
    return (deep_output, deep_grad / deep_scale, mid_grad / mid_scale)


def solution(mesh):
    in_specs = (P("dp", "space", None, None), P(), P(), P(), P("dp", "space", None, None, None))
    out_specs = (P("dp", "space", None, None, None), P(None, None, None, "space", None), P())
    return jax.shard_map(
        on_device, mesh=mesh, in_specs=in_specs, out_specs=out_specs, check_vma=False
    )
```

```python
import math

import jax
import jax.numpy as jnp
from jax import lax
from jax.sharding import PartitionSpec as P

SLOPE = 0.3


def padded_2(block, sides, width):
    for axis, dim in sides:
        count = lax.axis_size(axis)
        forward = [(i, i + 1) for i in range(count - 1)]
        backward = [(target, source) for source, target in forward]
        low = lax.ppermute(
            lax.slice_in_dim(block, block.shape[dim] - width, None, axis=dim), axis, forward
        )
        high = lax.ppermute(lax.slice_in_dim(block, 0, width, axis=dim), axis, backward)
        block = jnp.concatenate([low, block, high], axis=dim)
    return block


def digit_groups(axes, widest=4):
    groups = []
    for axis in axes:
        if widest == 2:
            groups += [(axis, 1 << k, 2) for k in range(lax.axis_size(axis).bit_length() - 1)]
            continue
        bits = lax.axis_size(axis).bit_length() - 1
        bit = 1
        if bits % 2 == 1:
            groups.append((axis, 1, 2))
            bit = 2
        while bit < lax.axis_size(axis):
            groups.append((axis, bit, 4))
            bit *= 4
    return groups


def xor_pairs(axis, flip):
    return [(i, i ^ flip) for i in range(lax.axis_size(axis))]


def exchange_parts(block, axis, bit, radix):
    digit = (lax.axis_index(axis) // bit) % radix
    size = block.shape[0]
    out = jnp.zeros((radix * size,) + block.shape[1:], block.dtype)
    out = lax.dynamic_update_slice_in_dim(out, block, digit * size, 0)
    for t in range(1, radix):
        got = lax.ppermute(block, axis, xor_pairs(axis, t * bit))
        out = lax.dynamic_update_slice_in_dim(out, got, (digit ^ t) * size, 0)
    return out


def gather_depth(block, axis):
    for _, bit, radix in digit_groups((axis,)):
        block = exchange_parts(block, axis, bit, radix)
    return block


def gather_for_kernel_grad(pooled, grad_pre, axis):
    count = lax.axis_size(axis)
    me = lax.axis_index(axis)
    width = pooled.shape[3] // count
    slab = pooled.shape[0]
    both = (count * slab,) + pooled.shape[1:3]
    columns = jnp.zeros(both + (width,), pooled.dtype)
    full = jnp.zeros(both + grad_pre.shape[3:], grad_pre.dtype)
    own = lax.dynamic_slice_in_dim(pooled, me * width, width, 3)
    columns = lax.dynamic_update_slice_in_dim(columns, own, me * slab, 0)
    full = lax.dynamic_update_slice_in_dim(full, grad_pre, me * slab, 0)
    for t in range(1, count):
        part = lax.dynamic_slice_in_dim(pooled, (me ^ t) * width, width, 3)
        got = lax.ppermute(jnp.concatenate([part, grad_pre], 3), axis, xor_pairs(axis, t))
        columns = lax.dynamic_update_slice_in_dim(columns, got[..., :width], (me ^ t) * slab, 0)
        full = lax.dynamic_update_slice_in_dim(full, got[..., width:], (me ^ t) * slab, 0)
    return columns, full


def reduce_all(rows, axes, wire_dtype, tied=(), widest=4):
    groups = digit_groups(axes, widest)
    count = rows.shape[0]
    parts = 1
    for _, _, radix in groups:
        parts *= radix
    held = jnp.pad(rows, ((0, -count % parts), (0, 0)))
    for step, (axis, bit, radix) in enumerate(groups):
        digit = (lax.axis_index(axis) // bit) % radix
        size = held.shape[0] // radix
        total = lax.dynamic_slice_in_dim(held, digit * size, size, 0)
        for t in range(1, radix):
            send = lax.dynamic_slice_in_dim(held, (digit ^ t) * size, size, 0)
            got = lax.ppermute(send.astype(wire_dtype), axis, xor_pairs(axis, t * bit))
            total = total + got.astype(held.dtype)
        held = total
        if step < len(tied):
            held, ready = lax.optimization_barrier((held, tied[step]))
            tied = tied[:step] + (ready,) + tied[step + 1 :]
    held = held.astype(wire_dtype)
    for axis, bit, radix in reversed(groups):
        held = exchange_parts(held, axis, bit, radix)
    return held[:count].astype(rows.dtype), tied


def activate(value):
    return SLOPE * value + (1.0 - SLOPE) * value * jax.nn.sigmoid(value)


def activate_slope(value):
    sig = jax.nn.sigmoid(value)
    return SLOPE + (1.0 - SLOPE) * (sig + value * sig * (1.0 - sig))


def conv_depth(padded, kernel):
    return lax.conv_general_dilated(
        padded[None],
        kernel,
        (1, 1, 1),
        [(0, 0), (1, 1), (1, 1)],
        dimension_numbers=("NDHWC", "DHWIO", "NDHWC"),
        preferred_element_type=jnp.float32,
    )[0]


def pool_cells(values):
    dd, hh, ww, cc = values.shape
    return values.reshape(dd // 2, 2, hh // 2, 2, ww // 2, 2, cc).mean(axis=(1, 3, 5))


def expand(values):
    return jnp.repeat(jnp.repeat(jnp.repeat(values, 2, 0), 2, 1), 2, 2)


def tap_terms(padded, cotangent, taps):
    dd, hh, ww, _ = cotangent.shape
    terms = []
    for tap in taps:
        depth_off, row_off, col_off = tap // 9, (tap // 3) % 3, tap % 3
        window = padded[
            depth_off : depth_off + dd, row_off : row_off + hh, col_off : col_off + ww
        ]
        terms.append(
            jnp.einsum("dhwi,dhwo->io", window, cotangent, preferred_element_type=jnp.float32)
        )
    return terms


def kernel_grad(padded, cotangent):
    terms = tap_terms(padded, cotangent, range(27))
    return jnp.stack(terms).reshape(3, 3, 3, padded.shape[-1], cotangent.shape[-1])


def pad_sides(values):
    return jnp.pad(values, ((0, 0), (1, 1), (1, 1), (0, 0)))


def pad_depth(values):
    return jnp.pad(values, ((1, 1), (0, 0), (0, 0), (0, 0)))


def pad_cells(values):
    return jnp.pad(values, ((1, 1), (1, 1), (1, 1), (0, 0)))


def on_device(volume, first_kernel, mid_kernel, deep_kernel, deep_cotangent):
    slab_depth = volume.shape[1]
    side_cells = volume.shape[2]
    in_channels = volume.shape[3] // side_cells
    space_count = lax.axis_size("space")
    space_index = lax.axis_index("space")
    input_field = volume[0].reshape(slab_depth, side_cells, side_cells, in_channels)
    padded = padded_2(input_field, (("space", 0),), 2)
    first_pre = conv_depth(padded, first_kernel)
    plane = space_index * slab_depth - 1 + jnp.arange(first_pre.shape[0])
    inside = ((plane >= 0) & (plane < space_count * slab_depth)).astype(jnp.float32)
    hidden = (activate(first_pre) * inside[:, None, None, None]).astype(jnp.bfloat16)
    pre_mid = conv_depth(hidden, mid_kernel)
    pooled = pool_cells(activate(pre_mid)).astype(jnp.bfloat16)
    pre_deep = conv_depth(padded_2(pooled, (("space", 0),), 1), deep_kernel)
    pooled, pre_deep = lax.optimization_barrier((pooled, pre_deep))
    cotangent = deep_cotangent[0].astype(jnp.float32)
    grad_pre = (cotangent * activate_slope(pre_deep)).astype(jnp.bfloat16)
    flipped = jnp.swapaxes(deep_kernel[::-1, ::-1, ::-1], 3, 4)
    pooled_grad = conv_depth(padded_2(grad_pre, (("space", 0),), 1), flipped).astype(jnp.bfloat16)
    grad_pre, pooled_grad, pooled = lax.optimization_barrier((grad_pre, pooled_grad, pooled))
    columns, all_grad_pre = gather_for_kernel_grad(pooled, grad_pre, "space")
    grad_mid = (expand(pooled_grad.astype(jnp.float32)) * 0.125 * activate_slope(pre_mid)).astype(
        jnp.bfloat16
    )
    mid_term = kernel_grad(pad_sides(hidden), grad_mid)
    mid_shape = mid_term.shape
    inputs = (columns, all_grad_pre)
    mid_grad, (early, late) = reduce_all(
        mid_term.reshape(-1, mid_shape[-1]), ("dp", "space"), jnp.float32, (inputs, inputs)
    )
    mid_grad = mid_grad.reshape(mid_shape)
    terms = tap_terms(pad_cells(early[0]), early[1], range(14))
    terms += tap_terms(pad_cells(late[0]), late[1], range(14, 27))
    deep_term = jnp.stack(terms).reshape(3, 3, 3, columns.shape[-1], all_grad_pre.shape[-1])
    deep_shape = deep_term.shape
    deep_grad, _ = reduce_all(deep_term.reshape(-1, deep_shape[-1]), ("dp",), jnp.bfloat16, (), 2)
    deep_grad = deep_grad.reshape(deep_shape)
    device_total = lax.axis_size("dp") * space_count
    cell_count = slab_depth * side_cells * side_cells
    deep_scale = math.sqrt(device_total * cell_count // 8)
    mid_scale = math.sqrt(device_total * cell_count)
    deep_output = activate(pre_deep).astype(jnp.bfloat16)[None]
    return (deep_output, deep_grad / deep_scale, mid_grad / mid_scale)


def solution(mesh):
    in_specs = (P("dp", "space", None, None), P(), P(), P(), P("dp", "space", None, None, None))
    out_specs = (P("dp", "space", None, None, None), P(None, None, None, "space", None), P())
    return jax.shard_map(
        on_device, mesh=mesh, in_specs=in_specs, out_specs=out_specs, check_vma=False
    )
```

```python
import math

import jax
import jax.numpy as jnp
from jax import lax
from jax.sharding import PartitionSpec as P

SLOPE = 0.3


def padded_2(block, sides, width):
    for axis, dim in sides:
        count = lax.axis_size(axis)
        forward = [(i, i + 1) for i in range(count - 1)]
        backward = [(target, source) for source, target in forward]
        low = lax.ppermute(
            lax.slice_in_dim(block, block.shape[dim] - width, None, axis=dim), axis, forward
        )
        high = lax.ppermute(lax.slice_in_dim(block, 0, width, axis=dim), axis, backward)
        block = jnp.concatenate([low, block, high], axis=dim)
    return block


def digit_groups(axes):
    groups = []
    for axis in axes:
        bits = lax.axis_size(axis).bit_length() - 1
        bit = 1
        if bits % 2 == 1:
            groups.append((axis, 1, 2))
            bit = 2
        while bit < lax.axis_size(axis):
            groups.append((axis, bit, 4))
            bit *= 4
    return groups


def xor_pairs(axis, flip):
    return [(i, i ^ flip) for i in range(lax.axis_size(axis))]


def exchange_parts(block, axis, bit, radix):
    digit = (lax.axis_index(axis) // bit) % radix
    size = block.shape[0]
    out = jnp.zeros((radix * size,) + block.shape[1:], block.dtype)
    out = lax.dynamic_update_slice_in_dim(out, block, digit * size, 0)
    for t in range(1, radix):
        got = lax.ppermute(block, axis, xor_pairs(axis, t * bit))
        out = lax.dynamic_update_slice_in_dim(out, got, (digit ^ t) * size, 0)
    return out


def gather_depth(block, axis):
    for _, bit, radix in digit_groups((axis,)):
        block = exchange_parts(block, axis, bit, radix)
    return block


def gather_for_kernel_grad(pooled, grad_pre, axis):
    count = lax.axis_size(axis)
    me = lax.axis_index(axis)
    width = pooled.shape[3] // count
    slab = pooled.shape[0]
    both = (count * slab,) + pooled.shape[1:3]
    columns = jnp.zeros(both + (width,), pooled.dtype)
    full = jnp.zeros(both + grad_pre.shape[3:], grad_pre.dtype)
    own = lax.dynamic_slice_in_dim(pooled, me * width, width, 3)
    columns = lax.dynamic_update_slice_in_dim(columns, own, me * slab, 0)
    full = lax.dynamic_update_slice_in_dim(full, grad_pre, me * slab, 0)
    for t in range(1, count):
        part = lax.dynamic_slice_in_dim(pooled, (me ^ t) * width, width, 3)
        got = lax.ppermute(jnp.concatenate([part, grad_pre], 3), axis, xor_pairs(axis, t))
        columns = lax.dynamic_update_slice_in_dim(columns, got[..., :width], (me ^ t) * slab, 0)
        full = lax.dynamic_update_slice_in_dim(full, got[..., width:], (me ^ t) * slab, 0)
    return columns, full


def reduce_all(rows, axes, wire_dtype, tied=()):
    groups = digit_groups(axes)
    count = rows.shape[0]
    parts = 1
    for _, _, radix in groups:
        parts *= radix
    held = jnp.pad(rows, ((0, -count % parts), (0, 0)))
    for step, (axis, bit, radix) in enumerate(groups):
        digit = (lax.axis_index(axis) // bit) % radix
        size = held.shape[0] // radix
        total = lax.dynamic_slice_in_dim(held, digit * size, size, 0)
        for t in range(1, radix):
            send = lax.dynamic_slice_in_dim(held, (digit ^ t) * size, size, 0)
            got = lax.ppermute(send.astype(wire_dtype), axis, xor_pairs(axis, t * bit))
            total = total + got.astype(held.dtype)
        held = total
        if step < len(tied):
            held, ready = lax.optimization_barrier((held, tied[step]))
            tied = tied[:step] + (ready,) + tied[step + 1 :]
    held = held.astype(wire_dtype)
    for axis, bit, radix in reversed(groups):
        held = exchange_parts(held, axis, bit, radix)
    return held[:count].astype(rows.dtype), tied


def activate(value):
    return SLOPE * value + (1.0 - SLOPE) * value * jax.nn.sigmoid(value)


def activate_slope(value):
    sig = jax.nn.sigmoid(value)
    return SLOPE + (1.0 - SLOPE) * (sig + value * sig * (1.0 - sig))


def conv_depth(padded, kernel):
    return lax.conv_general_dilated(
        padded[None],
        kernel,
        (1, 1, 1),
        [(0, 0), (1, 1), (1, 1)],
        dimension_numbers=("NDHWC", "DHWIO", "NDHWC"),
        preferred_element_type=jnp.float32,
    )[0]


def pool_cells(values):
    dd, hh, ww, cc = values.shape
    return values.reshape(dd // 2, 2, hh // 2, 2, ww // 2, 2, cc).mean(axis=(1, 3, 5))


def expand(values):
    return jnp.repeat(jnp.repeat(jnp.repeat(values, 2, 0), 2, 1), 2, 2)


def tap_terms(padded, cotangent, taps):
    dd, hh, ww, _ = cotangent.shape
    terms = []
    for tap in taps:
        depth_off, row_off, col_off = tap // 9, (tap // 3) % 3, tap % 3
        window = padded[
            depth_off : depth_off + dd, row_off : row_off + hh, col_off : col_off + ww
        ]
        terms.append(
            jnp.einsum("dhwi,dhwo->io", window, cotangent, preferred_element_type=jnp.float32)
        )
    return terms


def kernel_grad(padded, cotangent):
    terms = tap_terms(padded, cotangent, range(27))
    return jnp.stack(terms).reshape(3, 3, 3, padded.shape[-1], cotangent.shape[-1])


def kernel_grad_shifted(values, padded_cotangent):
    dd, hh, ww = padded_cotangent.shape[0], values.shape[1], values.shape[2]
    tap_list = []
    for depth_off in range(3):
        for row_off in range(3):
            for col_off in range(3):
                window = padded_cotangent[
                    :, 2 - row_off : 2 - row_off + hh, 2 - col_off : 2 - col_off + ww
                ]
                tap_list.append(
                    jnp.einsum(
                        "dhwi,dhwo->io",
                        values[depth_off : depth_off + dd],
                        window,
                        preferred_element_type=jnp.float32,
                    )
                )
    return jnp.stack(tap_list).reshape(3, 3, 3, values.shape[-1], padded_cotangent.shape[-1])


def pad_sides(values):
    return jnp.pad(values, ((0, 0), (1, 1), (1, 1), (0, 0)))


def pad_depth(values):
    return jnp.pad(values, ((1, 1), (0, 0), (0, 0), (0, 0)))


def pad_cells(values):
    return jnp.pad(values, ((1, 1), (1, 1), (1, 1), (0, 0)))


def on_device(volume, first_kernel, mid_kernel, deep_kernel, deep_cotangent):
    slab_depth = volume.shape[1]
    side_cells = volume.shape[2]
    in_channels = volume.shape[3] // side_cells
    space_count = lax.axis_size("space")
    space_index = lax.axis_index("space")
    input_field = volume[0].reshape(slab_depth, side_cells, side_cells, in_channels)
    padded = padded_2(input_field, (("space", 0),), 2)
    first_pre = conv_depth(padded, first_kernel)
    plane = space_index * slab_depth - 1 + jnp.arange(first_pre.shape[0])
    inside = ((plane >= 0) & (plane < space_count * slab_depth)).astype(jnp.float32)
    hidden = (activate(first_pre) * inside[:, None, None, None]).astype(jnp.bfloat16)
    pre_mid = conv_depth(hidden, mid_kernel)
    pooled = pool_cells(activate(pre_mid)).astype(jnp.bfloat16)
    pre_deep = conv_depth(padded_2(pooled, (("space", 0),), 1), deep_kernel)
    pooled, pre_deep = lax.optimization_barrier((pooled, pre_deep))
    cotangent = deep_cotangent[0].astype(jnp.float32)
    grad_pre = (cotangent * activate_slope(pre_deep)).astype(jnp.bfloat16)
    flipped = jnp.swapaxes(deep_kernel[::-1, ::-1, ::-1], 3, 4)
    pooled_grad = conv_depth(padded_2(grad_pre, (("space", 0),), 1), flipped).astype(jnp.bfloat16)
    grad_pre, pooled_grad, pooled = lax.optimization_barrier((grad_pre, pooled_grad, pooled))
    columns, all_grad_pre = gather_for_kernel_grad(pooled, grad_pre, "space")
    grad_mid = (expand(pooled_grad.astype(jnp.float32)) * 0.125 * activate_slope(pre_mid)).astype(
        jnp.bfloat16
    )
    mid_term = kernel_grad_shifted(hidden, pad_sides(grad_mid))
    mid_shape = mid_term.shape
    inputs = (columns, all_grad_pre)
    mid_grad, (early, late) = reduce_all(
        mid_term.reshape(-1, mid_shape[-1]), ("dp", "space"), jnp.float32, (inputs, inputs)
    )
    mid_grad = mid_grad.reshape(mid_shape)
    terms = tap_terms(pad_cells(early[0]), early[1], range(14))
    terms += tap_terms(pad_cells(late[0]), late[1], range(14, 27))
    deep_term = jnp.stack(terms).reshape(3, 3, 3, columns.shape[-1], all_grad_pre.shape[-1])
    deep_shape = deep_term.shape
    deep_grad, _ = reduce_all(deep_term.reshape(-1, deep_shape[-1]), ("dp",), jnp.bfloat16)
    deep_grad = deep_grad.reshape(deep_shape)
    device_total = lax.axis_size("dp") * space_count
    cell_count = slab_depth * side_cells * side_cells
    deep_scale = math.sqrt(device_total * cell_count // 8)
    mid_scale = math.sqrt(device_total * cell_count)
    deep_output = activate(pre_deep).astype(jnp.bfloat16)[None]
    return (deep_output, deep_grad / deep_scale, mid_grad / mid_scale)


def solution(mesh):
    in_specs = (P("dp", "space", None, None), P(), P(), P(), P("dp", "space", None, None, None))
    out_specs = (P("dp", "space", None, None, None), P(None, None, None, "space", None), P())
    return jax.shard_map(
        on_device, mesh=mesh, in_specs=in_specs, out_specs=out_specs, check_vma=False
    )
```

```python
import math

import jax
import jax.numpy as jnp
from jax import lax
from jax.sharding import PartitionSpec as P

SLOPE = 0.3


def padded_2(block, sides, width):
    for axis, dim in sides:
        count = lax.axis_size(axis)
        forward = [(i, i + 1) for i in range(count - 1)]
        backward = [(target, source) for source, target in forward]
        low = lax.ppermute(
            lax.slice_in_dim(block, block.shape[dim] - width, None, axis=dim), axis, forward
        )
        high = lax.ppermute(lax.slice_in_dim(block, 0, width, axis=dim), axis, backward)
        block = jnp.concatenate([low, block, high], axis=dim)
    return block


def digit_groups(axes):
    groups = []
    for axis in axes:
        bits = lax.axis_size(axis).bit_length() - 1
        bit = 1
        if bits % 2 == 1:
            groups.append((axis, 1, 2))
            bit = 2
        while bit < lax.axis_size(axis):
            groups.append((axis, bit, 4))
            bit *= 4
    return groups


def xor_pairs(axis, flip):
    return [(i, i ^ flip) for i in range(lax.axis_size(axis))]


def exchange_parts(block, axis, bit, radix):
    digit = (lax.axis_index(axis) // bit) % radix
    size = block.shape[0]
    out = jnp.zeros((radix * size,) + block.shape[1:], block.dtype)
    out = lax.dynamic_update_slice_in_dim(out, block, digit * size, 0)
    for t in range(1, radix):
        got = lax.ppermute(block, axis, xor_pairs(axis, t * bit))
        out = lax.dynamic_update_slice_in_dim(out, got, (digit ^ t) * size, 0)
    return out


def gather_depth(block, axis):
    for _, bit, radix in digit_groups((axis,)):
        block = exchange_parts(block, axis, bit, radix)
    return block


def gather_for_kernel_grad(pooled, grad_pre, axis):
    count = lax.axis_size(axis)
    me = lax.axis_index(axis)
    width = pooled.shape[3] // count
    slab = pooled.shape[0]
    both = (count * slab,) + pooled.shape[1:3]
    columns = jnp.zeros(both + (width,), pooled.dtype)
    full = jnp.zeros(both + grad_pre.shape[3:], grad_pre.dtype)
    own = lax.dynamic_slice_in_dim(pooled, me * width, width, 3)
    columns = lax.dynamic_update_slice_in_dim(columns, own, me * slab, 0)
    full = lax.dynamic_update_slice_in_dim(full, grad_pre, me * slab, 0)
    for t in range(1, count):
        part = lax.dynamic_slice_in_dim(pooled, (me ^ t) * width, width, 3)
        got = lax.ppermute(jnp.concatenate([part, grad_pre], 3), axis, xor_pairs(axis, t))
        columns = lax.dynamic_update_slice_in_dim(columns, got[..., :width], (me ^ t) * slab, 0)
        full = lax.dynamic_update_slice_in_dim(full, got[..., width:], (me ^ t) * slab, 0)
    return columns, full


def reduce_all(rows, axes, wire_dtype, tied=()):
    groups = digit_groups(axes)
    count = rows.shape[0]
    parts = 1
    for _, _, radix in groups:
        parts *= radix
    held = jnp.pad(rows, ((0, -count % parts), (0, 0)))
    for step, (axis, bit, radix) in enumerate(groups):
        digit = (lax.axis_index(axis) // bit) % radix
        size = held.shape[0] // radix
        total = lax.dynamic_slice_in_dim(held, digit * size, size, 0)
        for t in range(1, radix):
            send = lax.dynamic_slice_in_dim(held, (digit ^ t) * size, size, 0)
            got = lax.ppermute(send.astype(wire_dtype), axis, xor_pairs(axis, t * bit))
            total = total + got.astype(held.dtype)
        held = total
        if step < len(tied):
            held, ready = lax.optimization_barrier((held, tied[step]))
            tied = tied[:step] + (ready,) + tied[step + 1 :]
    held = held.astype(wire_dtype)
    for axis, bit, radix in reversed(groups):
        held = exchange_parts(held, axis, bit, radix)
    return held[:count].astype(rows.dtype), tied


def activate(value):
    return SLOPE * value + (1.0 - SLOPE) * value * jax.nn.sigmoid(value)


def activate_slope(value):
    sig = jax.nn.sigmoid(value)
    return SLOPE + (1.0 - SLOPE) * (sig + value * sig * (1.0 - sig))


def conv_depth(padded, kernel):
    return lax.conv_general_dilated(
        padded[None],
        kernel,
        (1, 1, 1),
        [(0, 0), (1, 1), (1, 1)],
        dimension_numbers=("NDHWC", "DHWIO", "NDHWC"),
        preferred_element_type=jnp.float32,
    )[0]


def pool_cells(values):
    dd, hh, ww, cc = values.shape
    return values.reshape(dd // 2, 2, hh // 2, 2, ww // 2, 2, cc).mean(axis=(1, 3, 5))


def expand(values):
    return jnp.repeat(jnp.repeat(jnp.repeat(values, 2, 0), 2, 1), 2, 2)


def tap_terms(padded, cotangent, taps):
    dd, hh, ww, _ = cotangent.shape
    terms = []
    for tap in taps:
        depth_off, row_off, col_off = tap // 9, (tap // 3) % 3, tap % 3
        window = padded[
            depth_off : depth_off + dd, row_off : row_off + hh, col_off : col_off + ww
        ]
        terms.append(
            jnp.einsum("dhwi,dhwo->io", window, cotangent, preferred_element_type=jnp.float32)
        )
    return terms


def kernel_grad(padded, cotangent):
    terms = tap_terms(padded, cotangent, range(27))
    return jnp.stack(terms).reshape(3, 3, 3, padded.shape[-1], cotangent.shape[-1])


def pad_sides(values):
    return jnp.pad(values, ((0, 0), (1, 1), (1, 1), (0, 0)))


def pad_depth(values):
    return jnp.pad(values, ((1, 1), (0, 0), (0, 0), (0, 0)))


def pad_cells(values):
    return jnp.pad(values, ((1, 1), (1, 1), (1, 1), (0, 0)))


def on_device(volume, first_kernel, mid_kernel, deep_kernel, deep_cotangent):
    slab_depth = volume.shape[1]
    side_cells = volume.shape[2]
    in_channels = volume.shape[3] // side_cells
    space_count = lax.axis_size("space")
    space_index = lax.axis_index("space")
    halo_field = padded_2(volume[0], (("space", 0),), 2)
    padded = halo_field.reshape(slab_depth + 4, side_cells, side_cells, in_channels)
    first_pre = conv_depth(padded, first_kernel)
    plane = space_index * slab_depth - 1 + jnp.arange(first_pre.shape[0])
    inside = ((plane >= 0) & (plane < space_count * slab_depth)).astype(jnp.float32)
    hidden = (activate(first_pre) * inside[:, None, None, None]).astype(jnp.bfloat16)
    pre_mid = conv_depth(hidden, mid_kernel)
    pooled = pool_cells(activate(pre_mid)).astype(jnp.bfloat16)
    pre_deep = conv_depth(padded_2(pooled, (("space", 0),), 1), deep_kernel)
    pooled, pre_deep = lax.optimization_barrier((pooled, pre_deep))
    cotangent = deep_cotangent[0].astype(jnp.float32)
    grad_pre = (cotangent * activate_slope(pre_deep)).astype(jnp.bfloat16)
    flipped = jnp.swapaxes(deep_kernel[::-1, ::-1, ::-1], 3, 4)
    pooled_grad = conv_depth(padded_2(grad_pre, (("space", 0),), 1), flipped).astype(jnp.bfloat16)
    grad_pre, pooled_grad, pooled = lax.optimization_barrier((grad_pre, pooled_grad, pooled))
    columns, all_grad_pre = gather_for_kernel_grad(pooled, grad_pre, "space")
    grad_mid = (expand(pooled_grad.astype(jnp.float32)) * 0.125 * activate_slope(pre_mid)).astype(
        jnp.bfloat16
    )
    mid_term = kernel_grad(pad_sides(hidden), grad_mid)
    mid_shape = mid_term.shape
    inputs = (columns, all_grad_pre)
    mid_grad, (early, late) = reduce_all(
        mid_term.reshape(-1, mid_shape[-1]), ("dp", "space"), jnp.float32, (inputs, inputs)
    )
    mid_grad = mid_grad.reshape(mid_shape)
    terms = tap_terms(pad_cells(early[0]), early[1], range(14))
    terms += tap_terms(pad_cells(late[0]), late[1], range(14, 27))
    deep_term = jnp.stack(terms).reshape(3, 3, 3, columns.shape[-1], all_grad_pre.shape[-1])
    deep_shape = deep_term.shape
    deep_grad, _ = reduce_all(deep_term.reshape(-1, deep_shape[-1]), ("dp",), jnp.bfloat16)
    deep_grad = deep_grad.reshape(deep_shape)
    device_total = lax.axis_size("dp") * space_count
    cell_count = slab_depth * side_cells * side_cells
    deep_scale = math.sqrt(device_total * cell_count // 8)
    mid_scale = math.sqrt(device_total * cell_count)
    deep_output = activate(pre_deep).astype(jnp.bfloat16)[None]
    return (deep_output, deep_grad / deep_scale, mid_grad / mid_scale)


def solution(mesh):
    in_specs = (P("dp", "space", None, None), P(), P(), P(), P("dp", "space", None, None, None))
    out_specs = (P("dp", "space", None, None, None), P(None, None, None, "space", None), P())
    return jax.shard_map(
        on_device, mesh=mesh, in_specs=in_specs, out_specs=out_specs, check_vma=False
    )
```

```python
import math

import jax
import jax.numpy as jnp
from jax import lax
from jax.sharding import PartitionSpec as P

SLOPE = 0.3


def padded_2(block, sides, width):
    for axis, dim in sides:
        count = lax.axis_size(axis)
        forward = [(i, i + 1) for i in range(count - 1)]
        backward = [(target, source) for source, target in forward]
        low = lax.ppermute(
            lax.slice_in_dim(block, block.shape[dim] - width, None, axis=dim), axis, forward
        )
        high = lax.ppermute(lax.slice_in_dim(block, 0, width, axis=dim), axis, backward)
        block = jnp.concatenate([low, block, high], axis=dim)
    return block


def digit_groups(axes):
    groups = []
    for axis in axes:
        bits = lax.axis_size(axis).bit_length() - 1
        bit = 1
        if bits % 2 == 1:
            groups.append((axis, 1, 2))
            bit = 2
        while bit < lax.axis_size(axis):
            groups.append((axis, bit, 4))
            bit *= 4
    return groups


def xor_pairs(axis, flip):
    return [(i, i ^ flip) for i in range(lax.axis_size(axis))]


def exchange_parts(block, axis, bit, radix):
    digit = (lax.axis_index(axis) // bit) % radix
    size = block.shape[0]
    out = jnp.zeros((radix * size,) + block.shape[1:], block.dtype)
    out = lax.dynamic_update_slice_in_dim(out, block, digit * size, 0)
    for t in range(1, radix):
        got = lax.ppermute(block, axis, xor_pairs(axis, t * bit))
        out = lax.dynamic_update_slice_in_dim(out, got, (digit ^ t) * size, 0)
    return out


def gather_depth(block, axis):
    for _, bit, radix in digit_groups((axis,)):
        block = exchange_parts(block, axis, bit, radix)
    return block


def gather_for_kernel_grad(pooled, grad_pre, axis):
    count = lax.axis_size(axis)
    me = lax.axis_index(axis)
    width = pooled.shape[3] // count
    slab = pooled.shape[0]
    both = (count * slab,) + pooled.shape[1:3]
    columns = jnp.zeros(both + (width,), pooled.dtype)
    full = jnp.zeros(both + grad_pre.shape[3:], grad_pre.dtype)
    own = lax.dynamic_slice_in_dim(pooled, me * width, width, 3)
    columns = lax.dynamic_update_slice_in_dim(columns, own, me * slab, 0)
    full = lax.dynamic_update_slice_in_dim(full, grad_pre, me * slab, 0)
    for t in range(1, count):
        part = lax.dynamic_slice_in_dim(pooled, (me ^ t) * width, width, 3)
        got = lax.ppermute(jnp.concatenate([part, grad_pre], 3), axis, xor_pairs(axis, t))
        columns = lax.dynamic_update_slice_in_dim(columns, got[..., :width], (me ^ t) * slab, 0)
        full = lax.dynamic_update_slice_in_dim(full, got[..., width:], (me ^ t) * slab, 0)
    return columns, full


def reduce_all(rows, axes, wire_dtype, tied=()):
    groups = digit_groups(axes)
    count = rows.shape[0]
    parts = 1
    for _, _, radix in groups:
        parts *= radix
    held = jnp.pad(rows, ((0, -count % parts), (0, 0)))
    for step, (axis, bit, radix) in enumerate(groups):
        digit = (lax.axis_index(axis) // bit) % radix
        size = held.shape[0] // radix
        total = lax.dynamic_slice_in_dim(held, digit * size, size, 0)
        for t in range(1, radix):
            send = lax.dynamic_slice_in_dim(held, (digit ^ t) * size, size, 0)
            got = lax.ppermute(send.astype(wire_dtype), axis, xor_pairs(axis, t * bit))
            total = total + got.astype(held.dtype)
        held = total
        if step < len(tied):
            held, ready = lax.optimization_barrier((held, tied[step]))
            tied = tied[:step] + (ready,) + tied[step + 1 :]
    held = held.astype(wire_dtype)
    for axis, bit, radix in reversed(groups):
        held = exchange_parts(held, axis, bit, radix)
    return held[:count].astype(rows.dtype), tied


def activate(value):
    return SLOPE * value + (1.0 - SLOPE) * value * jax.nn.sigmoid(value)


def activate_slope(value):
    sig = jax.nn.sigmoid(value)
    return SLOPE + (1.0 - SLOPE) * (sig + value * sig * (1.0 - sig))


def conv_depth(padded, kernel):
    return lax.conv_general_dilated(
        padded[None],
        kernel,
        (1, 1, 1),
        [(0, 0), (1, 1), (1, 1)],
        dimension_numbers=("NDHWC", "DHWIO", "NDHWC"),
        preferred_element_type=jnp.float32,
    )[0]


def pool_cells(values):
    dd, hh, ww, cc = values.shape
    return values.reshape(dd // 2, 2, hh // 2, 2, ww // 2, 2, cc).mean(axis=(1, 3, 5))


def expand(values):
    return jnp.repeat(jnp.repeat(jnp.repeat(values, 2, 0), 2, 1), 2, 2)


def tap_terms(padded, cotangent, taps):
    dd, hh, ww, _ = cotangent.shape
    terms = []
    for tap in taps:
        depth_off, row_off, col_off = tap // 9, (tap // 3) % 3, tap % 3
        window = padded[
            depth_off : depth_off + dd, row_off : row_off + hh, col_off : col_off + ww
        ]
        terms.append(
            jnp.einsum("dhwi,dhwo->io", window, cotangent, preferred_element_type=jnp.float32)
        )
    return terms


def shifted_terms(values, padded_cotangent, taps):
    dd, hh, ww, _ = values.shape
    terms = []
    for tap in taps:
        depth_off, row_off, col_off = tap // 9, (tap // 3) % 3, tap % 3
        window = padded_cotangent[
            2 - depth_off : 2 - depth_off + dd,
            2 - row_off : 2 - row_off + hh,
            2 - col_off : 2 - col_off + ww,
        ]
        terms.append(
            jnp.einsum("dhwi,dhwo->io", values, window, preferred_element_type=jnp.float32)
        )
    return terms


def kernel_grad(padded, cotangent):
    terms = tap_terms(padded, cotangent, range(27))
    return jnp.stack(terms).reshape(3, 3, 3, padded.shape[-1], cotangent.shape[-1])


def pad_sides(values):
    return jnp.pad(values, ((0, 0), (1, 1), (1, 1), (0, 0)))


def pad_depth(values):
    return jnp.pad(values, ((1, 1), (0, 0), (0, 0), (0, 0)))


def pad_cells(values):
    return jnp.pad(values, ((1, 1), (1, 1), (1, 1), (0, 0)))


def on_device(volume, first_kernel, mid_kernel, deep_kernel, deep_cotangent):
    slab_depth = volume.shape[1]
    side_cells = volume.shape[2]
    in_channels = volume.shape[3] // side_cells
    space_count = lax.axis_size("space")
    space_index = lax.axis_index("space")
    input_field = volume[0].reshape(slab_depth, side_cells, side_cells, in_channels)
    padded = padded_2(input_field, (("space", 0),), 2)
    first_pre = conv_depth(padded, first_kernel)
    plane = space_index * slab_depth - 1 + jnp.arange(first_pre.shape[0])
    inside = ((plane >= 0) & (plane < space_count * slab_depth)).astype(jnp.float32)
    hidden = (activate(first_pre) * inside[:, None, None, None]).astype(jnp.bfloat16)
    pre_mid = conv_depth(hidden, mid_kernel)
    pooled = pool_cells(activate(pre_mid)).astype(jnp.bfloat16)
    pre_deep = conv_depth(padded_2(pooled, (("space", 0),), 1), deep_kernel)
    pooled, pre_deep = lax.optimization_barrier((pooled, pre_deep))
    cotangent = deep_cotangent[0].astype(jnp.float32)
    grad_pre = (cotangent * activate_slope(pre_deep)).astype(jnp.bfloat16)
    flipped = jnp.swapaxes(deep_kernel[::-1, ::-1, ::-1], 3, 4)
    pooled_grad = conv_depth(padded_2(grad_pre, (("space", 0),), 1), flipped).astype(jnp.bfloat16)
    grad_pre, pooled_grad, pooled = lax.optimization_barrier((grad_pre, pooled_grad, pooled))
    columns, all_grad_pre = gather_for_kernel_grad(pooled, grad_pre, "space")
    grad_mid = (expand(pooled_grad.astype(jnp.float32)) * 0.125 * activate_slope(pre_mid)).astype(
        jnp.bfloat16
    )
    mid_term = kernel_grad(pad_sides(hidden), grad_mid)
    mid_shape = mid_term.shape
    inputs = (columns, all_grad_pre)
    mid_grad, (early, late) = reduce_all(
        mid_term.reshape(-1, mid_shape[-1]), ("dp", "space"), jnp.float32, (inputs, inputs)
    )
    mid_grad = mid_grad.reshape(mid_shape)
    terms = shifted_terms(early[0], pad_cells(early[1]), range(14))
    terms += shifted_terms(late[0], pad_cells(late[1]), range(14, 27))
    deep_term = jnp.stack(terms).reshape(3, 3, 3, columns.shape[-1], all_grad_pre.shape[-1])
    deep_shape = deep_term.shape
    deep_grad, _ = reduce_all(deep_term.reshape(-1, deep_shape[-1]), ("dp",), jnp.bfloat16)
    deep_grad = deep_grad.reshape(deep_shape)
    device_total = lax.axis_size("dp") * space_count
    cell_count = slab_depth * side_cells * side_cells
    deep_scale = math.sqrt(device_total * cell_count // 8)
    mid_scale = math.sqrt(device_total * cell_count)
    deep_output = activate(pre_deep).astype(jnp.bfloat16)[None]
    return (deep_output, deep_grad / deep_scale, mid_grad / mid_scale)


def solution(mesh):
    in_specs = (P("dp", "space", None, None), P(), P(), P(), P("dp", "space", None, None, None))
    out_specs = (P("dp", "space", None, None, None), P(None, None, None, "space", None), P())
    return jax.shard_map(
        on_device, mesh=mesh, in_specs=in_specs, out_specs=out_specs, check_vma=False
    )
```

```python
import math

import jax
import jax.numpy as jnp
from jax import lax
from jax.sharding import PartitionSpec as P

SLOPE = 0.3


def padded_2(block, sides, width):
    for axis, dim in sides:
        count = lax.axis_size(axis)
        forward = [(i, i + 1) for i in range(count - 1)]
        backward = [(target, source) for source, target in forward]
        low = lax.ppermute(
            lax.slice_in_dim(block, block.shape[dim] - width, None, axis=dim), axis, forward
        )
        high = lax.ppermute(lax.slice_in_dim(block, 0, width, axis=dim), axis, backward)
        block = jnp.concatenate([low, block, high], axis=dim)
    return block


def digit_groups(axes):
    groups = []
    for axis in axes:
        bits = lax.axis_size(axis).bit_length() - 1
        bit = 1
        if bits % 2 == 1:
            groups.append((axis, 1, 2))
            bit = 2
        while bit < lax.axis_size(axis):
            groups.append((axis, bit, 4))
            bit *= 4
    return groups


def xor_pairs(axis, flip):
    return [(i, i ^ flip) for i in range(lax.axis_size(axis))]


def exchange_parts(block, axis, bit, radix):
    digit = (lax.axis_index(axis) // bit) % radix
    size = block.shape[0]
    out = jnp.zeros((radix * size,) + block.shape[1:], block.dtype)
    out = lax.dynamic_update_slice_in_dim(out, block, digit * size, 0)
    for t in range(1, radix):
        got = lax.ppermute(block, axis, xor_pairs(axis, t * bit))
        out = lax.dynamic_update_slice_in_dim(out, got, (digit ^ t) * size, 0)
    return out


def gather_depth(block, axis):
    for _, bit, radix in digit_groups((axis,)):
        block = exchange_parts(block, axis, bit, radix)
    return block


def gather_for_kernel_grad(pooled, grad_pre, axis):
    count = lax.axis_size(axis)
    me = lax.axis_index(axis)
    width = pooled.shape[3] // count
    slab = pooled.shape[0]
    both = (count * slab,) + pooled.shape[1:3]
    columns = jnp.zeros(both + (width,), pooled.dtype)
    full = jnp.zeros(both + grad_pre.shape[3:], grad_pre.dtype)
    own = lax.dynamic_slice_in_dim(pooled, me * width, width, 3)
    columns = lax.dynamic_update_slice_in_dim(columns, own, me * slab, 0)
    full = lax.dynamic_update_slice_in_dim(full, grad_pre, me * slab, 0)
    for t in range(1, count):
        part = lax.dynamic_slice_in_dim(pooled, (me ^ t) * width, width, 3)
        got = lax.ppermute(jnp.concatenate([part, grad_pre], 3), axis, xor_pairs(axis, t))
        columns = lax.dynamic_update_slice_in_dim(columns, got[..., :width], (me ^ t) * slab, 0)
        full = lax.dynamic_update_slice_in_dim(full, got[..., width:], (me ^ t) * slab, 0)
    return columns, full


def reduce_all(rows, axes, wire_dtype, tied=()):
    groups = digit_groups(axes)
    count = rows.shape[0]
    parts = 1
    for _, _, radix in groups:
        parts *= radix
    held = jnp.pad(rows, ((0, -count % parts), (0, 0)))
    for step, (axis, bit, radix) in enumerate(groups):
        digit = (lax.axis_index(axis) // bit) % radix
        size = held.shape[0] // radix
        total = lax.dynamic_slice_in_dim(held, digit * size, size, 0)
        for t in range(1, radix):
            send = lax.dynamic_slice_in_dim(held, (digit ^ t) * size, size, 0)
            got = lax.ppermute(send.astype(wire_dtype), axis, xor_pairs(axis, t * bit))
            total = total + got.astype(held.dtype)
        held = total
        if step < len(tied):
            held, ready = lax.optimization_barrier((held, tied[step]))
            tied = tied[:step] + (ready,) + tied[step + 1 :]
    held = held.astype(wire_dtype)
    for axis, bit, radix in reversed(groups):
        held = exchange_parts(held, axis, bit, radix)
    return held[:count].astype(rows.dtype), tied


def activate(value):
    return SLOPE * value + (1.0 - SLOPE) * value * jax.nn.sigmoid(value)


def activate_slope(value):
    sig = jax.nn.sigmoid(value)
    return SLOPE + (1.0 - SLOPE) * (sig + value * sig * (1.0 - sig))


def conv_depth(padded, kernel):
    return lax.conv_general_dilated(
        padded[None],
        kernel,
        (1, 1, 1),
        [(0, 0), (1, 1), (1, 1)],
        dimension_numbers=("NDHWC", "DHWIO", "NDHWC"),
        preferred_element_type=jnp.float32,
    )[0]


def pool_cells(values):
    dd, hh, ww, cc = values.shape
    return values.reshape(dd // 2, 2, hh // 2, 2, ww // 2, 2, cc).mean(axis=(1, 3, 5))


def expand(values):
    return jnp.repeat(jnp.repeat(jnp.repeat(values, 2, 0), 2, 1), 2, 2)


def tap_terms(padded, cotangent, taps):
    dd, hh, ww, _ = cotangent.shape
    terms = []
    for tap in taps:
        depth_off, row_off, col_off = tap // 9, (tap // 3) % 3, tap % 3
        window = padded[
            depth_off : depth_off + dd, row_off : row_off + hh, col_off : col_off + ww
        ]
        terms.append(
            jnp.einsum("dhwi,dhwo->io", window, cotangent, preferred_element_type=jnp.float32)
        )
    return terms


def kernel_grad(padded, cotangent):
    terms = tap_terms(padded, cotangent, range(27))
    return jnp.stack(terms).reshape(3, 3, 3, padded.shape[-1], cotangent.shape[-1])


def pad_sides(values):
    return jnp.pad(values, ((0, 0), (1, 1), (1, 1), (0, 0)))


def pad_depth(values):
    return jnp.pad(values, ((1, 1), (0, 0), (0, 0), (0, 0)))


def pad_cells(values):
    return jnp.pad(values, ((1, 1), (1, 1), (1, 1), (0, 0)))


def on_device(volume, first_kernel, mid_kernel, deep_kernel, deep_cotangent):
    slab_depth = volume.shape[1]
    side_cells = volume.shape[2]
    in_channels = volume.shape[3] // side_cells
    space_count = lax.axis_size("space")
    space_index = lax.axis_index("space")
    input_field = volume[0].reshape(slab_depth, side_cells, side_cells, in_channels)
    padded = padded_2(input_field, (("space", 0),), 2)
    first_pre = conv_depth(padded, first_kernel)
    plane = space_index * slab_depth - 1 + jnp.arange(first_pre.shape[0])
    inside = ((plane >= 0) & (plane < space_count * slab_depth)).astype(jnp.float32)
    hidden = (activate(first_pre) * inside[:, None, None, None]).astype(jnp.bfloat16)
    pre_mid = conv_depth(hidden, mid_kernel)
    pooled = pool_cells(activate(pre_mid)).astype(jnp.bfloat16)
    pre_deep = conv_depth(padded_2(pooled, (("space", 0),), 1), deep_kernel)
    pooled, pre_deep = lax.optimization_barrier((pooled, pre_deep))
    cotangent = deep_cotangent[0].astype(jnp.float32)
    grad_pre = (cotangent * activate_slope(pre_deep)).astype(jnp.bfloat16)
    flipped = jnp.swapaxes(deep_kernel[::-1, ::-1, ::-1], 3, 4)
    pooled_grad = conv_depth(padded_2(grad_pre, (("space", 0),), 1), flipped).astype(jnp.bfloat16)
    grad_pre, pooled_grad, pooled = lax.optimization_barrier((grad_pre, pooled_grad, pooled))
    columns, all_grad_pre = gather_for_kernel_grad(pooled, grad_pre, "space")
    grad_mid = (expand(pooled_grad.astype(jnp.float32)) * 0.125 * activate_slope(pre_mid)).astype(
        jnp.bfloat16
    )
    mid_term = kernel_grad(pad_sides(hidden), grad_mid)
    mid_shape = mid_term.shape
    inputs = (columns, all_grad_pre)
    mid_grad, (early, late) = reduce_all(
        mid_term.reshape(-1, mid_shape[-1]), ("dp", "space"), jnp.float32, (inputs, inputs)
    )
    mid_grad = mid_grad.reshape(mid_shape)
    terms = tap_terms(pad_cells(early[0]), early[1], range(9))
    terms += tap_terms(pad_cells(late[0]), late[1], range(9, 27))
    deep_term = jnp.stack(terms).reshape(3, 3, 3, columns.shape[-1], all_grad_pre.shape[-1])
    deep_shape = deep_term.shape
    deep_grad, _ = reduce_all(deep_term.reshape(-1, deep_shape[-1]), ("dp",), jnp.bfloat16)
    deep_grad = deep_grad.reshape(deep_shape)
    device_total = lax.axis_size("dp") * space_count
    cell_count = slab_depth * side_cells * side_cells
    deep_scale = math.sqrt(device_total * cell_count // 8)
    mid_scale = math.sqrt(device_total * cell_count)
    deep_output = activate(pre_deep).astype(jnp.bfloat16)[None]
    return (deep_output, deep_grad / deep_scale, mid_grad / mid_scale)


def solution(mesh):
    in_specs = (P("dp", "space", None, None), P(), P(), P(), P("dp", "space", None, None, None))
    out_specs = (P("dp", "space", None, None, None), P(None, None, None, "space", None), P())
    return jax.shard_map(
        on_device, mesh=mesh, in_specs=in_specs, out_specs=out_specs, check_vma=False
    )
```
